512 devices in a mesh: tile: 64 (over z, x), image: 2 (over y_hi), tensor: 4 (over y_lo, core).
Axes of the slice: x: 4, y: 4 (y_hi: 2, y_lo: 2; y = y_hi * 2 + y_lo), z: 16, core: 2. Of those that a mesh axis runs over, the one named last changes fastest.
Arguments:
- latent: bfloat16 [2, 256, 640, 128], P('image', 'tile', 'tensor'), may hold values from -8 to 8
- tile_slot: int32 [2, 64], replicated, may hold values from 0 to 63, each once within a row
- tile_count: int32 [2], replicated, may hold values from 16 to 64, as said below
- merge_num: int32 [1], replicated, may hold values from 3 to 13
- conv_ema: bfloat16 [3, 3, 4, 2, 80, 640], P(None, None, 'tensor', 'image'), may hold values from -0.078125 to 0.078125
- conv_adjusted: bfloat16 [3, 3, 4, 2, 80, 640], P(None, None, 'tensor', 'image'), may hold values from -0.078125 to 0.078125
- query_ema: bfloat16 [640, 512], P('image', 'tensor'), may hold values from -4 to 4
- query_adjusted: bfloat16 [640, 512], P('image', 'tensor'), may hold values from -4 to 4
- kv_ema: bfloat16 [640, 2, 512], P('image', None, 'tensor'), may hold values from -4 to 4
- kv_adjusted: bfloat16 [640, 2, 512], P('image', None, 'tensor'), may hold values from -4 to 4
- out_ema: bfloat16 [640, 512], P('tensor', 'image'), may hold values from -0.25 to 0.25
- out_adjusted: bfloat16 [640, 512], P('tensor', 'image'), may hold values from -0.25 to 0.25
- norm_gain: bfloat16 [640], replicated, may hold values from 0.099609375 to 1.8984375
Outputs:
- denoised: bfloat16 [2, 256, 640, 128], P('image', 'tile', 'tensor')
The draws below stay inside these ranges and needn't reach their ends.
Inputs may be any that keep to these rules, and one draw needn't show every extreme that they name: `tile_count`: the number of live tiles of each image; exactly one image has all 64 live, the others fewer. `tile_slot`: each row is a permutation of the tiles' vertical positions.
All inputs are finite; a program needn't handle non-finite values.
Results may differ from the reference program's by a relative error of at most 0.007.
The reference program's roundings to bfloat16 on the way count: a program that leaves them out, or rounds other values in their place, can miss the bound.
Values may be sent and summed in bfloat16 or wider, within the bound.
No kernel may reach another device: no remote copies, remote signals or barrier semaphores. Data moves between devices by JAX's collectives and lax.ppermute only.
A program may use at most 64 MiB of HBM per device.

```python
import jax
import jax.numpy as jnp
from jax import lax

C = 640
HEADS = 8
HD = 64
ROWS = 4
COLS = 128
POOL = 4
TILES = 64
IMAGES = 2
TOK_TILE = 32
ATT = 512
OUT_GROUP = 80
N_IMAGE = 2
N_TENSOR = 4


def draw_tile_count(key, part):
    first_key, second_key = jax.random.split(jax.random.fold_in(key, 7))
    lowest = max(TILES // 4, 1)
    counts = jax.random.randint(first_key, (IMAGES,), lowest, TILES)
    filled = jax.random.randint(second_key, (), 0, IMAGES)
    return jnp.where(jnp.arange(IMAGES) == filled, TILES, counts).astype(jnp.int32)


def shared_columns(key):
    return jax.random.truncated_normal(jax.random.fold_in(key, 101), -4.0, 4.0, (C, ATT), jnp.float32)


def head_levels(key):
    levels = jnp.exp(jax.random.uniform(jax.random.fold_in(key, 102), (HEADS,), jnp.float32, jnp.log(1.4), jnp.log(5.0)))
    return jnp.repeat(levels, HD)


def drawn_weight(key, own):
    common = shared_columns(key)
    private = jax.random.truncated_normal(jax.random.fold_in(key, own), -4.0, 4.0, (C, ATT), jnp.float32)
    mixed = 0.9 * common + 0.4359 * private
    return mixed * head_levels(key)[None, :] / jnp.sqrt(jnp.float32(C))


def drawn_values(key, own):
    entries = jax.random.truncated_normal(jax.random.fold_in(key, own), -4.0, 4.0, (C, ATT), jnp.float32)
    return entries / jnp.sqrt(jnp.float32(C))


def draw_query_ema(key, part):
    return drawn_weight(key, 201).astype(jnp.bfloat16)


def draw_query_adjusted(key, part):
    return drawn_weight(key, 202).astype(jnp.bfloat16)


def draw_kv_ema(key, part):
    return jnp.stack([drawn_weight(key, 203), drawn_values(key, 213)], axis=1).astype(jnp.bfloat16)


def draw_kv_adjusted(key, part):
    return jnp.stack([drawn_weight(key, 204), drawn_values(key, 214)], axis=1).astype(jnp.bfloat16)


def draw_latent(key, part):
    base = jax.random.fold_in(key, 301)
    noise_key, pattern_key, amp_key, pick_key = jax.random.split(base, 4)
    shape = (IMAGES, TILES * ROWS, C, COLS)
    noise = jax.random.truncated_normal(noise_key, -3.5, 3.5, shape, jnp.float32)
    amp = jnp.exp(jax.random.uniform(amp_key, (IMAGES, TILES), jnp.float32, jnp.log(2.0), jnp.log(4.0)))
    pattern = jax.random.uniform(pattern_key, (IMAGES, TILES, C), jnp.float32, -1.0, 1.0)
    planted_count = max(1, TILES // 16)
    ranks = jax.vmap(lambda one_key: jax.random.permutation(one_key, TILES))(jax.random.split(pick_key, IMAGES))
    planted = (ranks < planted_count).astype(jnp.float32)
    block = (amp * planted)[:, :, None] * pattern
    expanded = jnp.repeat(block, ROWS, axis=1)[:, :, :, None]
    return (noise + expanded).astype(jnp.bfloat16)


def shard_levels(stream_key, shape, cuts, low, top_value):
    def one(axis_at, blocks):
        draws = jax.random.uniform(jax.random.fold_in(jax.random.fold_in(stream_key, 6), axis_at), (blocks,), jnp.float32, low / len(cuts), top_value / len(cuts))
        return jnp.repeat(jnp.exp(draws), shape[axis_at] // blocks).reshape((-1,) + (1,) * (len(shape) - axis_at - 1))

    loudness = one(*cuts[0])
    for cut in cuts[1:]:
        loudness = loudness * one(*cut)
    return loudness


def gaussian(key, extent, deviation, most, shards=(), held_as=jnp.bfloat16):
    gain = shard_levels(key, extent, shards, -0.22, 0.18) if shards else 1.0
    array = jax.random.normal(key, extent, jnp.float32) * deviation * gain
    return jnp.minimum(jnp.maximum(array, -most), most).astype(held_as)


def setup_inputs(seed: int = 0) -> dict:
    arg_keys = jax.random.split(jax.random.key(seed), 14)
    return {
        "latent": draw_latent(jax.random.fold_in(arg_keys[13], 71), 0),
        "tile_slot": jax.vmap(lambda own: jax.random.permutation(own, TILES))(jax.random.split(arg_keys[1], IMAGES)).reshape((IMAGES, TILES)).astype(jnp.int32),
        "tile_count": draw_tile_count(jax.random.fold_in(arg_keys[13], 71), 0),
        "merge_num": jax.random.randint(arg_keys[3], (1,), 3, 14).astype(jnp.int32),
        "conv_ema": gaussian(arg_keys[4], (3, 3, N_TENSOR, N_IMAGE, OUT_GROUP, C), (9 * C) ** -0.5, 0.078125, ((2, 4), (3, 2))),
        "conv_adjusted": gaussian(arg_keys[5], (3, 3, N_TENSOR, N_IMAGE, OUT_GROUP, C), (9 * C) ** -0.5, 0.078125, ((2, 4), (3, 2))),
        "query_ema": draw_query_ema(jax.random.fold_in(arg_keys[13], 71), 0),
        "query_adjusted": draw_query_adjusted(jax.random.fold_in(arg_keys[13], 71), 0),
        "kv_ema": draw_kv_ema(jax.random.fold_in(arg_keys[13], 71), 0),
        "kv_adjusted": draw_kv_adjusted(jax.random.fold_in(arg_keys[13], 71), 0),
        "out_ema": gaussian(arg_keys[10], (C, ATT), ATT ** -0.5, 0.25, ((0, 4), (1, 2))),
        "out_adjusted": gaussian(arg_keys[11], (C, ATT), ATT ** -0.5, 0.25, ((0, 4), (1, 2))),
        "norm_gain": jnp.clip(1.0 + 0.18 * jax.random.normal(arg_keys[12], (C,), jnp.float32), 0.099609375, 1.8984375).astype(jnp.bfloat16),
    }


def blend(ema_part, adjusted_part, blend_ratio):
    base = ema_part.astype(jnp.float32)
    return (base + blend_ratio * (adjusted_part.astype(jnp.float32) - base)).astype(jnp.bfloat16)

def reference(latent, tile_slot, tile_count, merge_num, conv_ema, conv_adjusted, query_ema, query_adjusted, kv_ema, kv_adjusted, out_ema, out_adjusted, norm_gain):
    blend_ratio = merge_num[0].astype(jnp.float32) / 16.0
    conv_w = blend(conv_ema, conv_adjusted, blend_ratio).reshape(3, 3, C, C)
    conv_hwio = jnp.transpose(conv_w, (0, 1, 3, 2)).astype(jnp.float32)
    query_w = blend(query_ema, query_adjusted, blend_ratio)
    kv_w = blend(kv_ema, kv_adjusted, blend_ratio).reshape(C, 2 * ATT)
    out_w = jnp.transpose(blend(out_ema, out_adjusted, blend_ratio))
    gain_f = norm_gain.astype(jnp.float32)
    qscale = HD ** (-0.5)
    cells = ROWS * COLS
    results = []
    for image_index in range(IMAGES):
        feats = jnp.transpose(latent[image_index], (0, 2, 1))
        slot_row = tile_slot[image_index]
        live_count = tile_count[image_index]
        activated = jax.nn.silu(feats.astype(jnp.float32)).astype(jnp.bfloat16)
        tiled = activated.reshape(TILES, ROWS, COLS, C)
        by_slot = jnp.argsort(slot_row)
        keep = (jnp.arange(TILES) < live_count).astype(jnp.bfloat16)
        ordered = tiled[by_slot] * keep[:, None, None, None]
        field = ordered.reshape(TILES * ROWS, COLS, C).astype(jnp.float32)
        conv_out = lax.conv_general_dilated(field[None], conv_hwio, (1, 1), ((1, 1), (1, 1)), dimension_numbers=('NHWC', 'HWIO', 'NHWC'), precision=lax.Precision.HIGHEST)[0]
        conv_tiles = conv_out.reshape(TILES, ROWS, COLS, C)[slot_row]
        section = (feats.astype(jnp.float32).reshape(TILES, ROWS, COLS, C) + conv_tiles).astype(jnp.bfloat16)
        section_f = section.astype(jnp.float32)
        pooled = section_f.reshape(TILES, ROWS // POOL, POOL, COLS // POOL, POOL, C).mean(axis=(2, 4))
        pooled = pooled.astype(jnp.bfloat16).reshape(TILES * TOK_TILE, C)
        kv_rows = jnp.dot(pooled, kv_w, preferred_element_type=jnp.float32).astype(jnp.bfloat16)
        key_rows = kv_rows[:, :ATT].reshape(-1, HEADS, HD).astype(jnp.float32)
        value_rows = kv_rows[:, ATT:].reshape(-1, HEADS, HD).astype(jnp.float32)
        live_tile = slot_row < live_count
        key_live = jnp.repeat(live_tile, TOK_TILE)
        key_livef = key_live.astype(jnp.float32)

        def per_tile(inputs):
            tile_section, tile_live = inputs
            rows_f = tile_section.reshape(cells, C).astype(jnp.float32)
            root_mean = jnp.sqrt(lax.optimization_barrier(jnp.mean(rows_f * rows_f, axis=-1)) + 1e-06)
            normed = (rows_f * gain_f / root_mean[:, None]).astype(jnp.bfloat16)
            queries = (jnp.dot(normed, query_w, preferred_element_type=jnp.float32) * qscale).astype(jnp.bfloat16)
            queries = queries.reshape(cells, HEADS, HD).astype(jnp.float32)
            scores = jnp.einsum('qhd,khd->hqk', queries, key_rows)
            scores = jnp.where(key_live[None, None, :], scores, -1e+30)
            top = lax.optimization_barrier(jnp.max(scores, axis=-1, keepdims=True))
            expd = jnp.exp(scores - top) * key_livef[None, None, :]
            attn_weights = expd.astype(jnp.bfloat16).astype(jnp.float32)
            totals = lax.optimization_barrier(jnp.sum(expd, axis=-1))
            mixed = jnp.einsum('hqk,khd->qhd', attn_weights, value_rows) / jnp.transpose(totals)[:, :, None]
            attended = mixed.astype(jnp.bfloat16).reshape(cells, ATT)
            projected = jnp.dot(attended, out_w, preferred_element_type=jnp.float32)
            final = (rows_f + projected) * tile_live.astype(jnp.float32)
            return final.astype(jnp.bfloat16).reshape(ROWS, COLS, C)
        outputs = lax.map(per_tile, (section, live_tile))
        results.append(jnp.transpose(outputs.reshape(TILES * ROWS, COLS, C), (0, 2, 1)))
    return jnp.stack(results)
```

```python
import numpy as np
import jax
import jax.numpy as jnp
from jax import lax
from jax.sharding import Mesh
from jax.sharding import PartitionSpec as P

HD = 64
POOL = 4
TILE_AXES = ("tz", "tx")


def blend(ema_part, adjusted_part, blend_ratio):
    base = ema_part.astype(jnp.float32)
    return (base + blend_ratio * (adjusted_part.astype(jnp.float32) - base)).astype(jnp.bfloat16)


def convolve(field, kernel, row_padding):
    return lax.conv_general_dilated(
        field[None],
        kernel,
        (1, 1),
        (row_padding, (1, 1)),
        dimension_numbers=("NHCW", "HWOI", "NHCW"),
        preferred_element_type=jnp.float32,
    )[0]


def slot_lookup(tile_ids, slot_row):
    tile_total = slot_row.shape[0]
    matches = tile_ids[:, None] == jnp.arange(tile_total, dtype=jnp.int32)[None, :]
    return jnp.sum(jnp.where(matches, slot_row[None, :], 0), axis=1)


def image_pair(part, image_index, axis):
    other = lax.ppermute(part, "image", [(0, 1), (1, 0)])
    first = jnp.where(image_index == 0, part, other)
    second = jnp.where(image_index == 0, other, part)
    return jnp.concatenate([first, second], axis=axis)


def tile_gather(part):
    inner = lax.all_gather(part, "tx", axis=0, tiled=False)
    outer = lax.all_gather(inner, "tz", axis=0, tiled=False)
    return outer.reshape((-1,) + part.shape)


def on_device(
    latent,
    tile_slot,
    tile_count,
    merge_num,
    conv_ema,
    conv_adjusted,
    query_ema,
    query_adjusted,
    kv_ema,
    kv_adjusted,
    out_ema,
    out_adjusted,
    norm_gain,
):
    image_index = lax.axis_index("image")
    tile_index = lax.axis_index("tz") * lax.axis_size("tx") + lax.axis_index("tx")
    slot_row = lax.dynamic_index_in_dim(tile_slot, image_index, 0, keepdims=False)
    live_count = lax.dynamic_index_in_dim(tile_count, image_index, 0, keepdims=False)
    my_slot = lax.dynamic_index_in_dim(slot_row, tile_index, 0, keepdims=False)
    live_flag = (my_slot < live_count).astype(jnp.float32)
    blend_ratio = merge_num[0].astype(jnp.float32) / 16.0

    feats = latent[0]
    tile_rows, chan_shard, tile_cols = feats.shape
    activated = jax.nn.silu(feats.astype(jnp.float32)).astype(jnp.bfloat16)
    rim_rows = jnp.stack([activated[0], activated[-1]])
    shard_piece = tile_gather(rim_rows)

    conv_w = image_pair(blend(conv_ema, conv_adjusted, blend_ratio), image_index, 3)
    query_w = image_pair(blend(query_ema, query_adjusted, blend_ratio), image_index, 0)
    kv_w = image_pair(blend(kv_ema, kv_adjusted, blend_ratio), image_index, 0)
    out_w = image_pair(blend(out_ema, out_adjusted, blend_ratio), image_index, 1)
    conv_w = conv_w.reshape(3, 3, -1, conv_w.shape[-1])

    tile_total = shard_piece.shape[0]
    tiles = jnp.arange(tile_total, dtype=jnp.int32)
    upper_src = jnp.sum(jnp.where(slot_row == my_slot - 1, tiles, 0))
    lower_src = jnp.sum(jnp.where(slot_row == my_slot + 1, tiles, 0))
    has_upper = my_slot > 0
    has_lower = my_slot + 1 < live_count
    upper = lax.dynamic_index_in_dim(shard_piece, upper_src, 0, keepdims=False)[1]
    lower = lax.dynamic_index_in_dim(shard_piece, lower_src, 0, keepdims=False)[0]
    upper = jnp.where(has_upper, upper, jnp.zeros_like(upper))
    lower = jnp.where(has_lower, lower, jnp.zeros_like(lower))
    stacked = jnp.concatenate([upper[None], activated, lower[None]], axis=0)
    padded = lax.all_gather(stacked, "tensor", axis=1, tiled=True)
    conv_out = convolve(padded, conv_w, (0, 0))
    section = (feats.astype(jnp.float32) + conv_out).astype(jnp.bfloat16)
    section_full = lax.all_gather(section, "tensor", axis=1, tiled=True)
    channels = section_full.shape[1]
    cells = tile_rows * tile_cols
    section_f = section_full.astype(jnp.float32)
    rows_f = jnp.transpose(section_f, (0, 2, 1)).reshape(cells, channels)
    root_mean = jnp.sqrt(jnp.mean(rows_f * rows_f, axis=-1) + 1e-06)
    normed = (rows_f * norm_gain.astype(jnp.float32) / root_mean[:, None]).astype(jnp.bfloat16)
    queries = (jnp.dot(normed, query_w, preferred_element_type=jnp.float32) * HD ** (-0.5)).astype(
        jnp.bfloat16
    )
    att_shard = queries.shape[1]
    head_count = att_shard // HD
    pooled = section_f.reshape(tile_rows // POOL, POOL, channels, tile_cols // POOL, POOL).mean(
        axis=(1, 4)
    )
    tok_count = pooled.shape[0] * pooled.shape[2]
    pooled = jnp.transpose(pooled, (0, 2, 1)).astype(jnp.bfloat16).reshape(tok_count, channels)
    kv_flat = kv_w.reshape(channels, 2 * att_shard)
    kv_local = jnp.dot(pooled, kv_flat, preferred_element_type=jnp.float32).astype(jnp.bfloat16)
    kv_rows = tile_gather(kv_local).reshape(-1, 2 * att_shard)
    key_rows = kv_rows[:, :att_shard]
    key_total = key_rows.shape[0]
    key_tile = jnp.arange(key_total, dtype=jnp.int32) // tok_count
    key_live = slot_lookup(key_tile, slot_row) < live_count
    key_livef = key_live.astype(jnp.float32)
    key_heads = key_rows.reshape(key_total, head_count, HD)
    value_heads = kv_rows[:, att_shard:].reshape(key_total, head_count, HD)

    total_list, accum_list = [], []
    for head_index in range(head_count):
        scores = lax.dot_general(
            queries[:, head_index * HD:(head_index + 1) * HD],
            key_heads[:, head_index],
            (((1,), (1,)), ((), ())),
            preferred_element_type=jnp.float32,
        )
        scores = jnp.where(key_live[None, :], scores, -1e30)
        top = jnp.max(scores, axis=1)
        expd = jnp.exp(scores - top[:, None]) * key_livef[None, :]
        total_list.append(jnp.sum(expd, axis=1))
        accum_list.append(
            jnp.dot(
                expd.astype(jnp.bfloat16),
                value_heads[:, head_index],
                preferred_element_type=jnp.float32,
            )
        )
    totals = jnp.stack(total_list, axis=1)
    accum = jnp.stack(accum_list, axis=1)
    attended = (accum / totals[..., None]).astype(jnp.bfloat16).reshape(cells, att_shard)
    attended_full = lax.all_gather(attended, "tensor", axis=1, tiled=True)
    projected = lax.dot_general(
        out_w, attended_full, (((1,), (1,)), ((), ())), preferred_element_type=jnp.float32
    )
    projected = jnp.transpose(projected.reshape(chan_shard, tile_rows, tile_cols), (1, 0, 2))
    final = (section.astype(jnp.float32) + projected) * live_flag
    return final.astype(jnp.bfloat16).reshape(1, tile_rows, chan_shard, tile_cols)


def solution(mesh):
    tiles = mesh.shape["tile"]
    inner = 4 if tiles % 4 == 0 else 1
    devices = np.asarray(mesh.devices).reshape(
        (tiles // inner, inner, mesh.shape["image"], mesh.shape["tensor"])
    )
    split = Mesh(devices, ("tz", "tx", "image", "tensor"))
    placed = (
        P("image", TILE_AXES, "tensor", None),
        P(),
        P(),
        P(),
        P(None, None, "tensor", "image", None, None),
        P(None, None, "tensor", "image", None, None),
        P("image", "tensor"),
        P("image", "tensor"),
        P("image", None, "tensor"),
        P("image", None, "tensor"),
        P("tensor", "image"),
        P("tensor", "image"),
        P(),
    )
    return jax.shard_map(
        on_device,
        mesh=split,
        in_specs=placed,
        out_specs=P("image", TILE_AXES, "tensor", None),
        check_vma=False,
    )
```

```python
import numpy as np
import jax
import jax.numpy as jnp
from jax import lax
from jax.sharding import Mesh
from jax.sharding import PartitionSpec as P

HD = 64
POOL = 4
TILE_AXES = ("tz", "tx")


def blend(ema_part, adjusted_part, blend_ratio):
    base = ema_part.astype(jnp.float32)
    return (base + blend_ratio * (adjusted_part.astype(jnp.float32) - base)).astype(jnp.bfloat16)


def convolve(field, kernel, row_padding):
    return lax.conv_general_dilated(
        field[None],
        kernel,
        (1, 1),
        (row_padding, (1, 1)),
        dimension_numbers=("NHCW", "HWOI", "NHCW"),
        preferred_element_type=jnp.float32,
    )[0]


def slot_lookup(tile_ids, slot_row):
    tile_total = slot_row.shape[0]
    matches = tile_ids[:, None] == jnp.arange(tile_total, dtype=jnp.int32)[None, :]
    return jnp.sum(jnp.where(matches, slot_row[None, :], 0), axis=1)


def image_pair(part, image_index, axis):
    other = lax.ppermute(part, "image", [(0, 1), (1, 0)])
    first = jnp.where(image_index == 0, part, other)
    second = jnp.where(image_index == 0, other, part)
    return jnp.concatenate([first, second], axis=axis)


def owner_of(slot, slot_row):
    tiles = jnp.arange(slot_row.shape[0], dtype=jnp.int32)
    return jnp.sum(jnp.where(slot_row == slot, tiles, 0))


def halo_rows(rims, slot_row, my_slot, tz_i, tx_i, n_x):
    column = lax.all_gather(rims, "tz", axis=0, tiled=False)
    received = [None]
    for shift in range(1, n_x):
        dest_tile = tz_i * n_x + (tx_i + shift) % n_x
        dest_slot = lax.dynamic_index_in_dim(slot_row, dest_tile, 0, keepdims=False)
        up_src = owner_of(dest_slot - 1, slot_row)
        down_src = owner_of(dest_slot + 1, slot_row)
        up_part = lax.dynamic_index_in_dim(column, up_src // n_x, 0, keepdims=False)[1]
        down_part = lax.dynamic_index_in_dim(column, down_src // n_x, 0, keepdims=False)[0]
        up_part = jnp.where(up_src % n_x == tx_i, up_part, jnp.zeros_like(up_part))
        down_part = jnp.where(down_src % n_x == tx_i, down_part, jnp.zeros_like(down_part))
        chunk = jnp.stack([up_part, down_part])
        received.append(
            lax.ppermute(chunk, "tx", [(i, (i + shift) % n_x) for i in range(n_x)])
        )
    up_src = owner_of(my_slot - 1, slot_row)
    down_src = owner_of(my_slot + 1, slot_row)
    up_shift = (tx_i - up_src % n_x) % n_x
    down_shift = (tx_i - down_src % n_x) % n_x
    up_own = lax.dynamic_index_in_dim(column, up_src // n_x, 0, keepdims=False)[1]
    down_own = lax.dynamic_index_in_dim(column, down_src // n_x, 0, keepdims=False)[0]
    upper = lax.select_n(up_shift, up_own, *[piece[0] for piece in received[1:]])
    lower = lax.select_n(down_shift, down_own, *[piece[1] for piece in received[1:]])
    return upper, lower


def on_device(
    latent,
    tile_slot,
    tile_count,
    merge_num,
    conv_ema,
    conv_adjusted,
    query_ema,
    query_adjusted,
    kv_ema,
    kv_adjusted,
    out_ema,
    out_adjusted,
    norm_gain,
):
    image_index = lax.axis_index("image")
    tile_index = lax.axis_index("tz") * lax.axis_size("tx") + lax.axis_index("tx")
    slot_row = lax.dynamic_index_in_dim(tile_slot, image_index, 0, keepdims=False)
    live_count = lax.dynamic_index_in_dim(tile_count, image_index, 0, keepdims=False)
    my_slot = lax.dynamic_index_in_dim(slot_row, tile_index, 0, keepdims=False)
    live_flag = (my_slot < live_count).astype(jnp.float32)
    blend_ratio = merge_num[0].astype(jnp.float32) / 16.0

    feats = latent[0]
    tile_rows, chan_shard, tile_cols = feats.shape
    activated = jax.nn.silu(feats.astype(jnp.float32)).astype(jnp.bfloat16)
    rim_rows = jnp.stack([activated[0], activated[-1]])
    n_x = lax.axis_size("tx")
    upper, lower = halo_rows(
        rim_rows, slot_row, my_slot, lax.axis_index("tz"), lax.axis_index("tx"), n_x
    )

    conv_w = image_pair(blend(conv_ema, conv_adjusted, blend_ratio), image_index, 3)
    query_w = image_pair(blend(query_ema, query_adjusted, blend_ratio), image_index, 0)
    kv_w = image_pair(blend(kv_ema, kv_adjusted, blend_ratio), image_index, 0)
    out_w = image_pair(blend(out_ema, out_adjusted, blend_ratio), image_index, 1)
    conv_w = conv_w.reshape(3, 3, -1, conv_w.shape[-1])

    has_upper = my_slot > 0
    has_lower = my_slot + 1 < live_count
    upper = jnp.where(has_upper, upper, jnp.zeros_like(upper))
    lower = jnp.where(has_lower, lower, jnp.zeros_like(lower))
    stacked = jnp.concatenate([upper[None], activated, lower[None]], axis=0)
    padded = lax.all_gather(stacked, "tensor", axis=1, tiled=True)
    conv_out = convolve(padded, conv_w, (0, 0))
    section = (feats.astype(jnp.float32) + conv_out).astype(jnp.bfloat16)
    section_full = lax.all_gather(section, "tensor", axis=1, tiled=True)
    channels = section_full.shape[1]
    cells = tile_rows * tile_cols
    section_f = section_full.astype(jnp.float32)
    rows_f = jnp.transpose(section_f, (0, 2, 1)).reshape(cells, channels)
    root_mean = jnp.sqrt(jnp.mean(rows_f * rows_f, axis=-1) + 1e-06)
    normed = (rows_f * norm_gain.astype(jnp.float32) / root_mean[:, None]).astype(jnp.bfloat16)
    queries = (jnp.dot(normed, query_w, preferred_element_type=jnp.float32) * HD ** (-0.5)).astype(
        jnp.bfloat16
    )
    att_shard = queries.shape[1]
    head_count = att_shard // HD
    pooled = section_f.reshape(tile_rows // POOL, POOL, channels, tile_cols // POOL, POOL).mean(
        axis=(1, 4)
    )
    tok_count = pooled.shape[0] * pooled.shape[2]
    pooled = jnp.transpose(pooled, (0, 2, 1)).astype(jnp.bfloat16).reshape(tok_count, channels)
    kv_flat = kv_w.reshape(channels, 2 * att_shard)
    kv_local = jnp.dot(pooled, kv_flat, preferred_element_type=jnp.float32).astype(jnp.bfloat16)
    kv_column = lax.all_gather(kv_local, "tz", axis=0, tiled=False)
    kv_all = lax.all_gather(kv_column, "tx", axis=0, tiled=False)
    n_z = kv_all.shape[1]
    kv_rows = kv_all.reshape(-1, 2 * att_shard)
    key_rows = kv_rows[:, :att_shard]
    key_total = key_rows.shape[0]
    key_tile = (
        jnp.arange(n_x, dtype=jnp.int32)[:, None, None]
        + n_x * jnp.arange(n_z, dtype=jnp.int32)[None, :, None]
        + jnp.zeros((1, 1, tok_count), jnp.int32)
    ).reshape(-1)
    key_live = slot_lookup(key_tile, slot_row) < live_count
    key_livef = key_live.astype(jnp.float32)
    key_heads = key_rows.reshape(key_total, head_count, HD)
    value_heads = kv_rows[:, att_shard:].reshape(key_total, head_count, HD)

    total_list, accum_list = [], []
    for head_index in range(head_count):
        scores = lax.dot_general(
            queries[:, head_index * HD:(head_index + 1) * HD],
            key_heads[:, head_index],
            (((1,), (1,)), ((), ())),
            preferred_element_type=jnp.float32,
        )
        scores = jnp.where(key_live[None, :], scores, -1e30)
        top = jnp.max(scores, axis=1)
        expd = jnp.exp(scores - top[:, None]) * key_livef[None, :]
        total_list.append(jnp.sum(expd, axis=1))
        accum_list.append(
            jnp.dot(
                expd.astype(jnp.bfloat16),
                value_heads[:, head_index],
                preferred_element_type=jnp.float32,
            )
        )
    totals = jnp.stack(total_list, axis=1)
    accum = jnp.stack(accum_list, axis=1)
    attended = (accum / totals[..., None]).astype(jnp.bfloat16).reshape(cells, att_shard)
    attended_full = lax.all_gather(attended, "tensor", axis=1, tiled=True)
    projected = lax.dot_general(
        out_w, attended_full, (((1,), (1,)), ((), ())), preferred_element_type=jnp.float32
    )
    projected = jnp.transpose(projected.reshape(chan_shard, tile_rows, tile_cols), (1, 0, 2))
    final = (section.astype(jnp.float32) + projected) * live_flag
    return final.astype(jnp.bfloat16).reshape(1, tile_rows, chan_shard, tile_cols)


def solution(mesh):
    tiles = mesh.shape["tile"]
    inner = 4 if tiles % 4 == 0 else 1
    devices = np.asarray(mesh.devices).reshape(
        (tiles // inner, inner, mesh.shape["image"], mesh.shape["tensor"])
    )
    split = Mesh(devices, ("tz", "tx", "image", "tensor"))
    placed = (
        P("image", TILE_AXES, "tensor", None),
        P(),
        P(),
        P(),
        P(None, None, "tensor", "image", None, None),
        P(None, None, "tensor", "image", None, None),
        P("image", "tensor"),
        P("image", "tensor"),
        P("image", None, "tensor"),
        P("image", None, "tensor"),
        P("tensor", "image"),
        P("tensor", "image"),
        P(),
    )
    return jax.shard_map(
        on_device,
        mesh=split,
        in_specs=placed,
        out_specs=P("image", TILE_AXES, "tensor", None),
        check_vma=False,
    )
```

```python
import numpy as np
import jax
import jax.numpy as jnp
from jax import lax
from jax.sharding import Mesh
from jax.sharding import PartitionSpec as P

HD = 64
POOL = 4
TILE_AXES = ("zh", "zl", "tx")
PIECE_BYTES = 900 * 1024


def blend(ema_part, adjusted_part, blend_ratio):
    base = ema_part.astype(jnp.float32)
    return (base + blend_ratio * (adjusted_part.astype(jnp.float32) - base)).astype(jnp.bfloat16)


def convolve(field, kernel, row_padding):
    return lax.conv_general_dilated(
        field[None],
        kernel,
        (1, 1),
        (row_padding, (1, 1)),
        dimension_numbers=("NHCW", "HWOI", "NHCW"),
        preferred_element_type=jnp.float32,
    )[0]


def slot_lookup(tile_ids, slot_row):
    tile_total = slot_row.shape[0]
    matches = tile_ids[:, None] == jnp.arange(tile_total, dtype=jnp.int32)[None, :]
    return jnp.sum(jnp.where(matches, slot_row[None, :], 0), axis=1)


def image_pair(part, image_index, axis):
    other = lax.ppermute(part, "image", [(0, 1), (1, 0)])
    first = jnp.where(image_index == 0, part, other)
    second = jnp.where(image_index == 0, other, part)
    return jnp.concatenate([first, second], axis=axis)


def staged_gather(part, axes):
    out = part
    for axis in axes:
        size = lax.axis_size(axis)
        total = out.size * out.dtype.itemsize * size
        pieces = 1
        while total > PIECE_BYTES * pieces or out.shape[0] % pieces:
            pieces += 1
        if pieces == 1:
            out = lax.all_gather(out, axis, axis=0, tiled=False)
        else:
            step = out.shape[0] // pieces
            parts = [
                lax.all_gather(out[i * step:(i + 1) * step], axis, axis=1, tiled=False)
                for i in range(pieces)
            ]
            out = jnp.swapaxes(jnp.concatenate(parts, axis=0), 0, 1)
    return out


def owner_of(slot, slot_row):
    tiles = jnp.arange(slot_row.shape[0], dtype=jnp.int32)
    return jnp.sum(jnp.where(slot_row == slot, tiles, 0))


def halo_rows(rims, slot_row, my_slot, tz_i, tx_i, n_x):
    column = staged_gather(rims, ("zl", "zh")).reshape((-1,) + rims.shape)
    received = [None]
    for shift in range(1, n_x):
        dest_tile = tz_i * n_x + (tx_i + shift) % n_x
        dest_slot = lax.dynamic_index_in_dim(slot_row, dest_tile, 0, keepdims=False)
        up_src = owner_of(dest_slot - 1, slot_row)
        down_src = owner_of(dest_slot + 1, slot_row)
        up_part = lax.dynamic_index_in_dim(column, up_src // n_x, 0, keepdims=False)[1]
        down_part = lax.dynamic_index_in_dim(column, down_src // n_x, 0, keepdims=False)[0]
        up_part = jnp.where(up_src % n_x == tx_i, up_part, jnp.zeros_like(up_part))
        down_part = jnp.where(down_src % n_x == tx_i, down_part, jnp.zeros_like(down_part))
        chunk = jnp.stack([up_part, down_part])
        received.append(
            lax.ppermute(chunk, "tx", [(i, (i + shift) % n_x) for i in range(n_x)])
        )
    up_src = owner_of(my_slot - 1, slot_row)
    down_src = owner_of(my_slot + 1, slot_row)
    up_shift = (tx_i - up_src % n_x) % n_x
    down_shift = (tx_i - down_src % n_x) % n_x
    up_own = lax.dynamic_index_in_dim(column, up_src // n_x, 0, keepdims=False)[1]
    down_own = lax.dynamic_index_in_dim(column, down_src // n_x, 0, keepdims=False)[0]
    upper = lax.select_n(up_shift, up_own, *[piece[0] for piece in received[1:]])
    lower = lax.select_n(down_shift, down_own, *[piece[1] for piece in received[1:]])
    return upper, lower


def on_device(
    latent,
    tile_slot,
    tile_count,
    merge_num,
    conv_ema,
    conv_adjusted,
    query_ema,
    query_adjusted,
    kv_ema,
    kv_adjusted,
    out_ema,
    out_adjusted,
    norm_gain,
):
    image_index = lax.axis_index("image")
    z_index = lax.axis_index("zh") * lax.axis_size("zl") + lax.axis_index("zl")
    tile_index = z_index * lax.axis_size("tx") + lax.axis_index("tx")
    slot_row = lax.dynamic_index_in_dim(tile_slot, image_index, 0, keepdims=False)
    live_count = lax.dynamic_index_in_dim(tile_count, image_index, 0, keepdims=False)
    my_slot = lax.dynamic_index_in_dim(slot_row, tile_index, 0, keepdims=False)
    live_flag = (my_slot < live_count).astype(jnp.float32)
    blend_ratio = merge_num[0].astype(jnp.float32) / 16.0

    feats = latent[0]
    tile_rows, chan_shard, tile_cols = feats.shape
    activated = jax.nn.silu(feats.astype(jnp.float32)).astype(jnp.bfloat16)
    rim_rows = jnp.stack([activated[0], activated[-1]])
    n_x = lax.axis_size("tx")
    upper, lower = halo_rows(
        rim_rows, slot_row, my_slot, z_index, lax.axis_index("tx"), n_x
    )

    conv_w = image_pair(blend(conv_ema, conv_adjusted, blend_ratio), image_index, 3)
    query_w = image_pair(blend(query_ema, query_adjusted, blend_ratio), image_index, 0)
    kv_w = image_pair(blend(kv_ema, kv_adjusted, blend_ratio), image_index, 0)
    out_w = image_pair(blend(out_ema, out_adjusted, blend_ratio), image_index, 1)
    conv_w = conv_w.reshape(3, 3, -1, conv_w.shape[-1])

    has_upper = my_slot > 0
    has_lower = my_slot + 1 < live_count
    upper = jnp.where(has_upper, upper, jnp.zeros_like(upper))
    lower = jnp.where(has_lower, lower, jnp.zeros_like(lower))
    stacked = jnp.concatenate([upper[None], activated, lower[None]], axis=0)
    padded = lax.all_gather(stacked, "tensor", axis=1, tiled=True)
    conv_out = convolve(padded, conv_w, (0, 0))
    section = (feats.astype(jnp.float32) + conv_out).astype(jnp.bfloat16)
    section_full = lax.all_gather(section, "tensor", axis=1, tiled=True)
    channels = section_full.shape[1]
    cells = tile_rows * tile_cols
    section_f = section_full.astype(jnp.float32)
    rows_f = jnp.transpose(section_f, (0, 2, 1)).reshape(cells, channels)
    root_mean = jnp.sqrt(jnp.mean(rows_f * rows_f, axis=-1) + 1e-06)
    normed = (rows_f * norm_gain.astype(jnp.float32) / root_mean[:, None]).astype(jnp.bfloat16)
    queries = (jnp.dot(normed, query_w, preferred_element_type=jnp.float32) * HD ** (-0.5)).astype(
        jnp.bfloat16
    )
    att_shard = queries.shape[1]
    head_count = att_shard // HD
    pooled = section_f.reshape(tile_rows // POOL, POOL, channels, tile_cols // POOL, POOL).mean(
        axis=(1, 4)
    )
    tok_count = pooled.shape[0] * pooled.shape[2]
    pooled = jnp.transpose(pooled, (0, 2, 1)).astype(jnp.bfloat16).reshape(tok_count, channels)
    kv_flat = kv_w.reshape(channels, 2 * att_shard)
    kv_local = jnp.dot(pooled, kv_flat, preferred_element_type=jnp.float32).astype(jnp.bfloat16)
    kv_all = staged_gather(kv_local, ("zl", "zh", "tx"))
    n_z = kv_all.shape[1] * kv_all.shape[2]
    kv_rows = kv_all.reshape(-1, 2 * att_shard)
    key_rows = kv_rows[:, :att_shard]
    key_total = key_rows.shape[0]
    key_tile = (
        jnp.arange(n_x, dtype=jnp.int32)[:, None, None]
        + n_x * jnp.arange(n_z, dtype=jnp.int32)[None, :, None]
        + jnp.zeros((1, 1, tok_count), jnp.int32)
    ).reshape(-1)
    key_live = slot_lookup(key_tile, slot_row) < live_count
    key_livef = key_live.astype(jnp.float32)
    key_heads = key_rows.reshape(key_total, head_count, HD)
    value_heads = kv_rows[:, att_shard:].reshape(key_total, head_count, HD)

    total_list, accum_list = [], []
    for head_index in range(head_count):
        scores = lax.dot_general(
            queries[:, head_index * HD:(head_index + 1) * HD],
            key_heads[:, head_index],
            (((1,), (1,)), ((), ())),
            preferred_element_type=jnp.float32,
        )
        scores = jnp.where(key_live[None, :], scores, -1e30)
        top = jnp.max(scores, axis=1)
        expd = jnp.exp(scores - top[:, None]) * key_livef[None, :]
        total_list.append(jnp.sum(expd, axis=1))
        accum_list.append(
            jnp.dot(
                expd.astype(jnp.bfloat16),
                value_heads[:, head_index],
                preferred_element_type=jnp.float32,
            )
        )
    totals = jnp.stack(total_list, axis=1)
    accum = jnp.stack(accum_list, axis=1)
    attended = (accum / totals[..., None]).astype(jnp.bfloat16).reshape(cells, att_shard)
    attended_full = lax.all_gather(attended, "tensor", axis=1, tiled=True)
    projected = lax.dot_general(
        out_w, attended_full, (((1,), (1,)), ((), ())), preferred_element_type=jnp.float32
    )
    projected = jnp.transpose(projected.reshape(chan_shard, tile_rows, tile_cols), (1, 0, 2))
    final = (section.astype(jnp.float32) + projected) * live_flag
    return final.astype(jnp.bfloat16).reshape(1, tile_rows, chan_shard, tile_cols)


def solution(mesh):
    tiles = mesh.shape["tile"]
    inner = 4 if tiles % 4 == 0 else 1
    low = 4 if (tiles // inner) % 4 == 0 else 1
    devices = np.asarray(mesh.devices).reshape(
        (tiles // inner // low, low, inner, mesh.shape["image"], mesh.shape["tensor"])
    )
    split = Mesh(devices, ("zh", "zl", "tx", "image", "tensor"))
    placed = (
        P("image", TILE_AXES, "tensor", None),
        P(),
        P(),
        P(),
        P(None, None, "tensor", "image", None, None),
        P(None, None, "tensor", "image", None, None),
        P("image", "tensor"),
        P("image", "tensor"),
        P("image", None, "tensor"),
        P("image", None, "tensor"),
        P("tensor", "image"),
        P("tensor", "image"),
        P(),
    )
    return jax.shard_map(
        on_device,
        mesh=split,
        in_specs=placed,
        out_specs=P("image", TILE_AXES, "tensor", None),
        check_vma=False,
    )
```

```python
import numpy as np
import jax
import jax.numpy as jnp
from jax import lax
from jax.sharding import Mesh
from jax.sharding import PartitionSpec as P

HD = 64
POOL = 4
TILE_AXES = ("tz", "tx")


def blend(ema_part, adjusted_part, blend_ratio):
    base = ema_part.astype(jnp.float32)
    return (base + blend_ratio * (adjusted_part.astype(jnp.float32) - base)).astype(jnp.bfloat16)


def convolve(field, kernel, row_padding):
    return lax.conv_general_dilated(
        field[None],
        kernel,
        (1, 1),
        (row_padding, (1, 1)),
        dimension_numbers=("NHCW", "HWOI", "NHCW"),
        preferred_element_type=jnp.float32,
    )[0]


def slot_lookup(tile_ids, slot_row):
    tile_total = slot_row.shape[0]
    matches = tile_ids[:, None] == jnp.arange(tile_total, dtype=jnp.int32)[None, :]
    return jnp.sum(jnp.where(matches, slot_row[None, :], 0), axis=1)


def image_pair(part, image_index, axis):
    other = lax.ppermute(part, "image", [(0, 1), (1, 0)])
    first = jnp.where(image_index == 0, part, other)
    second = jnp.where(image_index == 0, other, part)
    return jnp.concatenate([first, second], axis=axis)


def owner_of(slot, slot_row):
    tiles = jnp.arange(slot_row.shape[0], dtype=jnp.int32)
    return jnp.sum(jnp.where(slot_row == slot, tiles, 0))


def halo_rows(rims, slot_row, my_slot, tz_i, tx_i, n_x):
    column = lax.all_gather(rims, "tz", axis=0, tiled=False)
    received = [None]
    for shift in range(1, n_x):
        dest_tile = tz_i * n_x + (tx_i + shift) % n_x
        dest_slot = lax.dynamic_index_in_dim(slot_row, dest_tile, 0, keepdims=False)
        up_src = owner_of(dest_slot - 1, slot_row)
        down_src = owner_of(dest_slot + 1, slot_row)
        up_part = lax.dynamic_index_in_dim(column, up_src // n_x, 0, keepdims=False)[1]
        down_part = lax.dynamic_index_in_dim(column, down_src // n_x, 0, keepdims=False)[0]
        up_part = jnp.where(up_src % n_x == tx_i, up_part, jnp.zeros_like(up_part))
        down_part = jnp.where(down_src % n_x == tx_i, down_part, jnp.zeros_like(down_part))
        chunk = jnp.stack([up_part, down_part])
        received.append(
            lax.ppermute(chunk, "tx", [(i, (i + shift) % n_x) for i in range(n_x)])
        )
    up_src = owner_of(my_slot - 1, slot_row)
    down_src = owner_of(my_slot + 1, slot_row)
    up_shift = (tx_i - up_src % n_x) % n_x
    down_shift = (tx_i - down_src % n_x) % n_x
    up_own = lax.dynamic_index_in_dim(column, up_src // n_x, 0, keepdims=False)[1]
    down_own = lax.dynamic_index_in_dim(column, down_src // n_x, 0, keepdims=False)[0]
    upper = lax.select_n(up_shift, up_own, *[piece[0] for piece in received[1:]])
    lower = lax.select_n(down_shift, down_own, *[piece[1] for piece in received[1:]])
    return upper, lower


def on_device(
    latent,
    tile_slot,
    tile_count,
    merge_num,
    conv_ema,
    conv_adjusted,
    query_ema,
    query_adjusted,
    kv_ema,
    kv_adjusted,
    out_ema,
    out_adjusted,
    norm_gain,
):
    image_index = lax.axis_index("image")
    tile_index = lax.axis_index("tz") * lax.axis_size("tx") + lax.axis_index("tx")
    slot_row = lax.dynamic_index_in_dim(tile_slot, image_index, 0, keepdims=False)
    live_count = lax.dynamic_index_in_dim(tile_count, image_index, 0, keepdims=False)
    my_slot = lax.dynamic_index_in_dim(slot_row, tile_index, 0, keepdims=False)
    live_flag = (my_slot < live_count).astype(jnp.float32)
    blend_ratio = merge_num[0].astype(jnp.float32) / 16.0

    feats = latent[0]
    tile_rows, chan_shard, tile_cols = feats.shape
    activated = jax.nn.silu(feats.astype(jnp.float32)).astype(jnp.bfloat16)
    rim_rows = jnp.stack([activated[0], activated[-1]])
    n_x = lax.axis_size("tx")
    upper, lower = halo_rows(
        rim_rows, slot_row, my_slot, lax.axis_index("tz"), lax.axis_index("tx"), n_x
    )

    conv_w = image_pair(blend(conv_ema, conv_adjusted, blend_ratio), image_index, 3)
    query_w = image_pair(blend(query_ema, query_adjusted, blend_ratio), image_index, 0)
    kv_w = image_pair(blend(kv_ema, kv_adjusted, blend_ratio), image_index, 0)
    out_w = image_pair(blend(out_ema, out_adjusted, blend_ratio), image_index, 1)
    conv_w = conv_w.reshape(3, 3, -1, conv_w.shape[-1])

    has_upper = my_slot > 0
    has_lower = my_slot + 1 < live_count
    upper = jnp.where(has_upper, upper, jnp.zeros_like(upper))
    lower = jnp.where(has_lower, lower, jnp.zeros_like(lower))
    block_full = lax.all_gather(activated, "tensor", axis=1, tiled=True)
    halo_full = lax.all_gather(jnp.stack([upper, lower]), "tensor", axis=1, tiled=True)
    padded = jnp.concatenate([halo_full[0:1], block_full, halo_full[1:2]], axis=0)
    conv_out = convolve(padded, conv_w, (0, 0))
    section = (feats.astype(jnp.float32) + conv_out).astype(jnp.bfloat16)
    section_full = lax.all_gather(section, "tensor", axis=1, tiled=True)
    channels = section_full.shape[1]
    cells = tile_rows * tile_cols
    section_f = section_full.astype(jnp.float32)
    rows_f = jnp.transpose(section_f, (0, 2, 1)).reshape(cells, channels)
    root_mean = jnp.sqrt(jnp.mean(rows_f * rows_f, axis=-1) + 1e-06)
    normed = (rows_f * norm_gain.astype(jnp.float32) / root_mean[:, None]).astype(jnp.bfloat16)
    queries = (jnp.dot(normed, query_w, preferred_element_type=jnp.float32) * HD ** (-0.5)).astype(
        jnp.bfloat16
    )
    att_shard = queries.shape[1]
    head_count = att_shard // HD
    pooled = section.astype(jnp.float32).reshape(
        tile_rows // POOL, POOL, chan_shard, tile_cols // POOL, POOL
    ).mean(axis=(1, 4))
    tok_count = pooled.shape[0] * pooled.shape[2]
    pooled = jnp.transpose(pooled, (0, 2, 1)).astype(jnp.bfloat16).reshape(tok_count, chan_shard)
    pooled = lax.all_gather(pooled, "tensor", axis=1, tiled=True)
    kv_flat = kv_w.reshape(channels, 2 * att_shard)
    kv_local = jnp.dot(pooled, kv_flat, preferred_element_type=jnp.float32).astype(jnp.bfloat16)
    kv_column = lax.all_gather(kv_local, "tz", axis=0, tiled=False)
    kv_all = lax.all_gather(kv_column, "tx", axis=0, tiled=False)
    n_z = kv_all.shape[1]
    kv_rows = kv_all.reshape(-1, 2 * att_shard)
    key_rows = kv_rows[:, :att_shard]
    key_total = key_rows.shape[0]
    key_tile = (
        jnp.arange(n_x, dtype=jnp.int32)[:, None, None]
        + n_x * jnp.arange(n_z, dtype=jnp.int32)[None, :, None]
        + jnp.zeros((1, 1, tok_count), jnp.int32)
    ).reshape(-1)
    key_live = slot_lookup(key_tile, slot_row) < live_count
    key_livef = key_live.astype(jnp.float32)
    key_heads = key_rows.reshape(key_total, head_count, HD)
    value_heads = kv_rows[:, att_shard:].reshape(key_total, head_count, HD)

    total_list, accum_list = [], []
    for head_index in range(head_count):
        scores = lax.dot_general(
            queries[:, head_index * HD:(head_index + 1) * HD],
            key_heads[:, head_index],
            (((1,), (1,)), ((), ())),
            preferred_element_type=jnp.float32,
        )
        scores = jnp.where(key_live[None, :], scores, -1e30)
        top = jnp.max(scores, axis=1)
        expd = jnp.exp(scores - top[:, None]) * key_livef[None, :]
        total_list.append(jnp.sum(expd, axis=1))
        accum_list.append(
            jnp.dot(
                expd.astype(jnp.bfloat16),
                value_heads[:, head_index],
                preferred_element_type=jnp.float32,
            )
        )
    totals = jnp.stack(total_list, axis=1)
    accum = jnp.stack(accum_list, axis=1)
    attended = (accum / totals[..., None]).astype(jnp.bfloat16).reshape(cells, att_shard)
    attended_full = lax.all_gather(attended, "tensor", axis=1, tiled=True)
    projected = lax.dot_general(
        out_w, attended_full, (((1,), (1,)), ((), ())), preferred_element_type=jnp.float32
    )
    projected = jnp.transpose(projected.reshape(chan_shard, tile_rows, tile_cols), (1, 0, 2))
    final = (section.astype(jnp.float32) + projected) * live_flag
    return final.astype(jnp.bfloat16).reshape(1, tile_rows, chan_shard, tile_cols)


def solution(mesh):
    tiles = mesh.shape["tile"]
    inner = 4 if tiles % 4 == 0 else 1
    devices = np.asarray(mesh.devices).reshape(
        (tiles // inner, inner, mesh.shape["image"], mesh.shape["tensor"])
    )
    split = Mesh(devices, ("tz", "tx", "image", "tensor"))
    placed = (
        P("image", TILE_AXES, "tensor", None),
        P(),
        P(),
        P(),
        P(None, None, "tensor", "image", None, None),
        P(None, None, "tensor", "image", None, None),
        P("image", "tensor"),
        P("image", "tensor"),
        P("image", None, "tensor"),
        P("image", None, "tensor"),
        P("tensor", "image"),
        P("tensor", "image"),
        P(),
    )
    return jax.shard_map(
        on_device,
        mesh=split,
        in_specs=placed,
        out_specs=P("image", TILE_AXES, "tensor", None),
        check_vma=False,
    )
```

```python
import numpy as np
import jax
import jax.numpy as jnp
from jax import lax
from jax.sharding import Mesh
from jax.sharding import PartitionSpec as P

HD = 64
POOL = 4
TILE_AXES = ("tz", "tx")


def blend(ema_part, adjusted_part, blend_ratio):
    base = ema_part.astype(jnp.float32)
    return (base + blend_ratio * (adjusted_part.astype(jnp.float32) - base)).astype(jnp.bfloat16)


def convolve(field, kernel, row_padding):
    return lax.conv_general_dilated(
        field[None],
        kernel,
        (1, 1),
        (row_padding, (1, 1)),
        dimension_numbers=("NHCW", "HWOI", "NHCW"),
        preferred_element_type=jnp.float32,
    )[0]


def slot_lookup(tile_ids, slot_row):
    tile_total = slot_row.shape[0]
    matches = tile_ids[:, None] == jnp.arange(tile_total, dtype=jnp.int32)[None, :]
    return jnp.sum(jnp.where(matches, slot_row[None, :], 0), axis=1)


def image_pair(part, image_index, axis):
    other = lax.ppermute(part, "image", [(0, 1), (1, 0)])
    first = jnp.where(image_index == 0, part, other)
    second = jnp.where(image_index == 0, other, part)
    return jnp.concatenate([first, second], axis=axis)


def owner_of(slot, slot_row):
    tiles = jnp.arange(slot_row.shape[0], dtype=jnp.int32)
    return jnp.sum(jnp.where(slot_row == slot, tiles, 0))


def halo_rows(rims, slot_row, my_slot, tz_i, tx_i, n_x):
    column = lax.all_gather(rims, "tz", axis=0, tiled=False)
    received = [None]
    for shift in range(1, n_x):
        dest_tile = tz_i * n_x + (tx_i + shift) % n_x
        dest_slot = lax.dynamic_index_in_dim(slot_row, dest_tile, 0, keepdims=False)
        up_src = owner_of(dest_slot - 1, slot_row)
        down_src = owner_of(dest_slot + 1, slot_row)
        up_part = lax.dynamic_index_in_dim(column, up_src // n_x, 0, keepdims=False)[1]
        down_part = lax.dynamic_index_in_dim(column, down_src // n_x, 0, keepdims=False)[0]
        up_part = jnp.where(up_src % n_x == tx_i, up_part, jnp.zeros_like(up_part))
        down_part = jnp.where(down_src % n_x == tx_i, down_part, jnp.zeros_like(down_part))
        chunk = jnp.stack([up_part, down_part])
        received.append(
            lax.ppermute(chunk, "tx", [(i, (i + shift) % n_x) for i in range(n_x)])
        )
    up_src = owner_of(my_slot - 1, slot_row)
    down_src = owner_of(my_slot + 1, slot_row)
    up_shift = (tx_i - up_src % n_x) % n_x
    down_shift = (tx_i - down_src % n_x) % n_x
    up_own = lax.dynamic_index_in_dim(column, up_src // n_x, 0, keepdims=False)[1]
    down_own = lax.dynamic_index_in_dim(column, down_src // n_x, 0, keepdims=False)[0]
    upper = lax.select_n(up_shift, up_own, *[piece[0] for piece in received[1:]])
    lower = lax.select_n(down_shift, down_own, *[piece[1] for piece in received[1:]])
    return upper, lower


def on_device(
    latent,
    tile_slot,
    tile_count,
    merge_num,
    conv_ema,
    conv_adjusted,
    query_ema,
    query_adjusted,
    kv_ema,
    kv_adjusted,
    out_ema,
    out_adjusted,
    norm_gain,
):
    image_index = lax.axis_index("image")
    tile_index = lax.axis_index("tz") * lax.axis_size("tx") + lax.axis_index("tx")
    slot_row = lax.dynamic_index_in_dim(tile_slot, image_index, 0, keepdims=False)
    live_count = lax.dynamic_index_in_dim(tile_count, image_index, 0, keepdims=False)
    my_slot = lax.dynamic_index_in_dim(slot_row, tile_index, 0, keepdims=False)
    live_flag = (my_slot < live_count).astype(jnp.float32)
    blend_ratio = merge_num[0].astype(jnp.float32) / 16.0

    feats = latent[0]
    tile_rows, chan_shard, tile_cols = feats.shape
    activated = jax.nn.silu(feats.astype(jnp.float32)).astype(jnp.bfloat16)
    rim_rows = jnp.stack([activated[0], activated[-1]])
    n_x = lax.axis_size("tx")
    upper, lower = halo_rows(
        rim_rows, slot_row, my_slot, lax.axis_index("tz"), lax.axis_index("tx"), n_x
    )

    conv_w = image_pair(blend(conv_ema, conv_adjusted, blend_ratio), image_index, 3)
    query_w = image_pair(blend(query_ema, query_adjusted, blend_ratio), image_index, 0)
    kv_w = image_pair(blend(kv_ema, kv_adjusted, blend_ratio), image_index, 0)
    out_w = image_pair(blend(out_ema, out_adjusted, blend_ratio), image_index, 1)
    conv_w = conv_w.reshape(3, 3, -1, conv_w.shape[-1])

    has_upper = my_slot > 0
    has_lower = my_slot + 1 < live_count
    upper = jnp.where(has_upper, upper, jnp.zeros_like(upper))
    lower = jnp.where(has_lower, lower, jnp.zeros_like(lower))
    block_full = lax.all_gather(activated, "tensor", axis=1, tiled=True)
    halo_full = lax.all_gather(jnp.stack([upper, lower]), "tensor", axis=1, tiled=True)
    padded = jnp.concatenate([halo_full[0:1], block_full, halo_full[1:2]], axis=0)
    conv_out = convolve(padded, conv_w, (0, 0))
    section_r = lax.reduce_precision(feats.astype(jnp.float32) + conv_out, exponent_bits=8, mantissa_bits=7)
    section = section_r.astype(jnp.bfloat16)
    section_full = lax.all_gather(section, "tensor", axis=1, tiled=True)
    channels = section_full.shape[1]
    cells = tile_rows * tile_cols
    section_f = section_full.astype(jnp.float32)
    rows_f = jnp.transpose(section_f, (0, 2, 1)).reshape(cells, channels)
    root_mean = jnp.sqrt(jnp.mean(rows_f * rows_f, axis=-1) + 1e-06)
    normed = (rows_f * norm_gain.astype(jnp.float32) / root_mean[:, None]).astype(jnp.bfloat16)
    queries = (jnp.dot(normed, query_w, preferred_element_type=jnp.float32) * HD ** (-0.5)).astype(
        jnp.bfloat16
    )
    att_shard = queries.shape[1]
    head_count = att_shard // HD
    pooled = section_r.reshape(
        tile_rows // POOL, POOL, chan_shard, tile_cols // POOL, POOL
    ).mean(axis=(1, 4))
    tok_count = pooled.shape[0] * pooled.shape[2]
    pooled = jnp.transpose(pooled, (0, 2, 1)).astype(jnp.bfloat16).reshape(tok_count, chan_shard)
    pooled = lax.all_gather(pooled, "tensor", axis=1, tiled=True)
    kv_flat = kv_w.reshape(channels, 2 * att_shard)
    kv_local = jnp.dot(pooled, kv_flat, preferred_element_type=jnp.float32).astype(jnp.bfloat16)
    kv_column = lax.all_gather(kv_local, "tz", axis=0, tiled=False)
    kv_all = lax.all_gather(kv_column, "tx", axis=0, tiled=False)
    n_z = kv_all.shape[1]
    kv_rows = kv_all.reshape(-1, 2 * att_shard)
    key_rows = kv_rows[:, :att_shard]
    key_total = key_rows.shape[0]
    key_tile = (
        jnp.arange(n_x, dtype=jnp.int32)[:, None, None]
        + n_x * jnp.arange(n_z, dtype=jnp.int32)[None, :, None]
        + jnp.zeros((1, 1, tok_count), jnp.int32)
    ).reshape(-1)
    key_live = slot_lookup(key_tile, slot_row) < live_count
    key_livef = key_live.astype(jnp.float32)
    key_heads = key_rows.reshape(key_total, head_count, HD)
    value_heads = kv_rows[:, att_shard:].reshape(key_total, head_count, HD)

    total_list, accum_list = [], []
    for head_index in range(head_count):
        scores = lax.dot_general(
            queries[:, head_index * HD:(head_index + 1) * HD],
            key_heads[:, head_index],
            (((1,), (1,)), ((), ())),
            preferred_element_type=jnp.float32,
        )
        scores = jnp.where(key_live[None, :], scores, -1e30)
        top = jnp.max(scores, axis=1)
        expd = jnp.exp(scores - top[:, None]) * key_livef[None, :]
        total_list.append(jnp.sum(expd, axis=1))
        accum_list.append(
            jnp.dot(
                expd.astype(jnp.bfloat16),
                value_heads[:, head_index],
                preferred_element_type=jnp.float32,
            )
        )
    totals = jnp.stack(total_list, axis=1)
    accum = jnp.stack(accum_list, axis=1)
    attended = (accum / totals[..., None]).astype(jnp.bfloat16).reshape(cells, att_shard)
    attended_full = lax.all_gather(attended, "tensor", axis=1, tiled=True)
    projected = lax.dot_general(
        out_w, attended_full, (((1,), (1,)), ((), ())), preferred_element_type=jnp.float32
    )
    projected = jnp.transpose(projected.reshape(chan_shard, tile_rows, tile_cols), (1, 0, 2))
    final = (section_r + projected) * live_flag
    return final.astype(jnp.bfloat16).reshape(1, tile_rows, chan_shard, tile_cols)


def solution(mesh):
    tiles = mesh.shape["tile"]
    inner = 4 if tiles % 4 == 0 else 1
    devices = np.asarray(mesh.devices).reshape(
        (tiles // inner, inner, mesh.shape["image"], mesh.shape["tensor"])
    )
    split = Mesh(devices, ("tz", "tx", "image", "tensor"))
    placed = (
        P("image", TILE_AXES, "tensor", None),
        P(),
        P(),
        P(),
        P(None, None, "tensor", "image", None, None),
        P(None, None, "tensor", "image", None, None),
        P("image", "tensor"),
        P("image", "tensor"),
        P("image", None, "tensor"),
        P("image", None, "tensor"),
        P("tensor", "image"),
        P("tensor", "image"),
        P(),
    )
    return jax.shard_map(
        on_device,
        mesh=split,
        in_specs=placed,
        out_specs=P("image", TILE_AXES, "tensor", None),
        check_vma=False,
    )
```

```python
import numpy as np
import jax
import jax.numpy as jnp
from jax import lax
from jax.sharding import Mesh
from jax.sharding import PartitionSpec as P

HD = 64
POOL = 4
TILE_AXES = ("zh", "zl", "tx")
Z_AXES = ("zh", "zl")


def blend(ema_part, adjusted_part, blend_ratio):
    base = ema_part.astype(jnp.float32)
    return (base + blend_ratio * (adjusted_part.astype(jnp.float32) - base)).astype(jnp.bfloat16)


def convolve(field, kernel, row_padding):
    return lax.conv_general_dilated(
        field[None],
        kernel,
        (1, 1),
        (row_padding, (1, 1)),
        dimension_numbers=("NHCW", "HWOI", "NHCW"),
        preferred_element_type=jnp.float32,
    )[0]


def slot_lookup(tile_ids, slot_row):
    tile_total = slot_row.shape[0]
    matches = tile_ids[:, None] == jnp.arange(tile_total, dtype=jnp.int32)[None, :]
    return jnp.sum(jnp.where(matches, slot_row[None, :], 0), axis=1)


def image_pair(part, image_index, axis):
    other = lax.ppermute(part, "image", [(0, 1), (1, 0)])
    first = jnp.where(image_index == 0, part, other)
    second = jnp.where(image_index == 0, other, part)
    return jnp.concatenate([first, second], axis=axis)


def owner_of(slot, slot_row):
    tiles = jnp.arange(slot_row.shape[0], dtype=jnp.int32)
    return jnp.sum(jnp.where(slot_row == slot, tiles, 0))


def halo_rows(rims, slot_row, my_slot, tz_i, tx_i, n_x):
    near = lax.all_gather(rims, "zl", axis=0, tiled=False)
    column = lax.all_gather(near, "zh", axis=0, tiled=False).reshape((-1,) + rims.shape)
    received = [None]
    for shift in range(1, n_x):
        dest_tile = tz_i * n_x + (tx_i + shift) % n_x
        dest_slot = lax.dynamic_index_in_dim(slot_row, dest_tile, 0, keepdims=False)
        up_src = owner_of(dest_slot - 1, slot_row)
        down_src = owner_of(dest_slot + 1, slot_row)
        up_part = lax.dynamic_index_in_dim(column, up_src // n_x, 0, keepdims=False)[1]
        down_part = lax.dynamic_index_in_dim(column, down_src // n_x, 0, keepdims=False)[0]
        up_part = jnp.where(up_src % n_x == tx_i, up_part, jnp.zeros_like(up_part))
        down_part = jnp.where(down_src % n_x == tx_i, down_part, jnp.zeros_like(down_part))
        chunk = jnp.stack([up_part, down_part])
        received.append(
            lax.ppermute(chunk, "tx", [(i, (i + shift) % n_x) for i in range(n_x)])
        )
    up_src = owner_of(my_slot - 1, slot_row)
    down_src = owner_of(my_slot + 1, slot_row)
    up_shift = (tx_i - up_src % n_x) % n_x
    down_shift = (tx_i - down_src % n_x) % n_x
    up_own = lax.dynamic_index_in_dim(column, up_src // n_x, 0, keepdims=False)[1]
    down_own = lax.dynamic_index_in_dim(column, down_src // n_x, 0, keepdims=False)[0]
    upper = lax.select_n(up_shift, up_own, *[piece[0] for piece in received[1:]])
    lower = lax.select_n(down_shift, down_own, *[piece[1] for piece in received[1:]])
    return upper, lower


def on_device(
    latent,
    tile_slot,
    tile_count,
    merge_num,
    conv_ema,
    conv_adjusted,
    query_ema,
    query_adjusted,
    kv_ema,
    kv_adjusted,
    out_ema,
    out_adjusted,
    norm_gain,
):
    image_index = lax.axis_index("image")
    z_index = lax.axis_index("zh") * lax.axis_size("zl") + lax.axis_index("zl")
    tile_index = z_index * lax.axis_size("tx") + lax.axis_index("tx")
    slot_row = lax.dynamic_index_in_dim(tile_slot, image_index, 0, keepdims=False)
    live_count = lax.dynamic_index_in_dim(tile_count, image_index, 0, keepdims=False)
    my_slot = lax.dynamic_index_in_dim(slot_row, tile_index, 0, keepdims=False)
    live_flag = (my_slot < live_count).astype(jnp.float32)
    blend_ratio = merge_num[0].astype(jnp.float32) / 16.0

    feats = latent[0]
    tile_rows, chan_shard, tile_cols = feats.shape
    activated = jax.nn.silu(feats.astype(jnp.float32)).astype(jnp.bfloat16)
    rim_rows = jnp.stack([activated[0], activated[-1]])
    n_x = lax.axis_size("tx")
    upper, lower = halo_rows(
        rim_rows, slot_row, my_slot, z_index, lax.axis_index("tx"), n_x
    )

    conv_w = image_pair(blend(conv_ema, conv_adjusted, blend_ratio), image_index, 3)
    query_w = image_pair(blend(query_ema, query_adjusted, blend_ratio), image_index, 0)
    kv_w = image_pair(blend(kv_ema, kv_adjusted, blend_ratio), image_index, 0)
    out_w = image_pair(blend(out_ema, out_adjusted, blend_ratio), image_index, 1)
    conv_w = conv_w.reshape(3, 3, -1, conv_w.shape[-1])

    has_upper = my_slot > 0
    has_lower = my_slot + 1 < live_count
    upper = jnp.where(has_upper, upper, jnp.zeros_like(upper))
    lower = jnp.where(has_lower, lower, jnp.zeros_like(lower))
    block_full = lax.all_gather(activated, "tensor", axis=1, tiled=True)
    halo_full = lax.all_gather(jnp.stack([upper, lower]), "tensor", axis=1, tiled=True)
    padded = jnp.concatenate([halo_full[0:1], block_full, halo_full[1:2]], axis=0)
    conv_out = convolve(padded, conv_w, (0, 0))
    section_r = lax.reduce_precision(feats.astype(jnp.float32) + conv_out, exponent_bits=8, mantissa_bits=7)
    section = section_r.astype(jnp.bfloat16)
    section_full = lax.all_gather(section, "tensor", axis=1, tiled=True)
    channels = section_full.shape[1]
    cells = tile_rows * tile_cols
    section_f = section_full.astype(jnp.float32)
    rows_f = jnp.transpose(section_f, (0, 2, 1)).reshape(cells, channels)
    root_mean = jnp.sqrt(jnp.mean(rows_f * rows_f, axis=-1) + 1e-06)
    normed = (rows_f * norm_gain.astype(jnp.float32) / root_mean[:, None]).astype(jnp.bfloat16)
    queries = (jnp.dot(normed, query_w, preferred_element_type=jnp.float32) * HD ** (-0.5)).astype(
        jnp.bfloat16
    )
    att_shard = queries.shape[1]
    head_count = att_shard // HD
    pooled = section_r.reshape(
        tile_rows // POOL, POOL, chan_shard, tile_cols // POOL, POOL
    ).mean(axis=(1, 4))
    tok_count = pooled.shape[0] * pooled.shape[2]
    pooled = jnp.transpose(pooled, (0, 2, 1)).astype(jnp.bfloat16).reshape(tok_count, chan_shard)
    pooled = lax.all_gather(pooled, "tensor", axis=1, tiled=True)
    kv_flat = kv_w.reshape(channels, 2 * att_shard)
    kv_local = jnp.dot(pooled, kv_flat, preferred_element_type=jnp.float32).astype(jnp.bfloat16)
    kv_column = lax.all_gather(kv_local, Z_AXES, axis=0, tiled=False)
    kv_all = lax.all_gather(kv_column, "tx", axis=0, tiled=False)
    n_z = kv_all.shape[1]
    kv_rows = kv_all.reshape(-1, 2 * att_shard)
    key_rows = kv_rows[:, :att_shard]
    key_total = key_rows.shape[0]
    key_tile = (
        jnp.arange(n_x, dtype=jnp.int32)[:, None, None]
        + n_x * jnp.arange(n_z, dtype=jnp.int32)[None, :, None]
        + jnp.zeros((1, 1, tok_count), jnp.int32)
    ).reshape(-1)
    key_live = slot_lookup(key_tile, slot_row) < live_count
    key_livef = key_live.astype(jnp.float32)
    key_heads = key_rows.reshape(key_total, head_count, HD)
    value_heads = kv_rows[:, att_shard:].reshape(key_total, head_count, HD)

    total_list, accum_list = [], []
    for head_index in range(head_count):
        scores = lax.dot_general(
            queries[:, head_index * HD:(head_index + 1) * HD],
            key_heads[:, head_index],
            (((1,), (1,)), ((), ())),
            preferred_element_type=jnp.float32,
        )
        scores = jnp.where(key_live[None, :], scores, -1e30)
        top = jnp.max(scores, axis=1)
        expd = jnp.exp(scores - top[:, None]) * key_livef[None, :]
        total_list.append(jnp.sum(expd, axis=1))
        accum_list.append(
            jnp.dot(
                expd.astype(jnp.bfloat16),
                value_heads[:, head_index],
                preferred_element_type=jnp.float32,
            )
        )
    totals = jnp.stack(total_list, axis=1)
    accum = jnp.stack(accum_list, axis=1)
    attended = (accum / totals[..., None]).astype(jnp.bfloat16).reshape(cells, att_shard)
    attended_full = lax.all_gather(attended, "tensor", axis=1, tiled=True)
    projected = lax.dot_general(
        out_w, attended_full, (((1,), (1,)), ((), ())), preferred_element_type=jnp.float32
    )
    projected = jnp.transpose(projected.reshape(chan_shard, tile_rows, tile_cols), (1, 0, 2))
    final = (section_r + projected) * live_flag
    return final.astype(jnp.bfloat16).reshape(1, tile_rows, chan_shard, tile_cols)


def solution(mesh):
    tiles = mesh.shape["tile"]
    inner = 4 if tiles % 4 == 0 else 1
    low = 4 if (tiles // inner) % 4 == 0 else 1
    devices = np.asarray(mesh.devices).reshape(
        (tiles // inner // low, low, inner, mesh.shape["image"], mesh.shape["tensor"])
    )
    split = Mesh(devices, ("zh", "zl", "tx", "image", "tensor"))
    placed = (
        P("image", TILE_AXES, "tensor", None),
        P(),
        P(),
        P(),
        P(None, None, "tensor", "image", None, None),
        P(None, None, "tensor", "image", None, None),
        P("image", "tensor"),
        P("image", "tensor"),
        P("image", None, "tensor"),
        P("image", None, "tensor"),
        P("tensor", "image"),
        P("tensor", "image"),
        P(),
    )
    return jax.shard_map(
        on_device,
        mesh=split,
        in_specs=placed,
        out_specs=P("image", TILE_AXES, "tensor", None),
        check_vma=False,
    )
```

```python
import numpy as np
import jax
import jax.numpy as jnp
from jax import lax
from jax.sharding import Mesh
from jax.sharding import PartitionSpec as P

HD = 64
POOL = 4
TILE_AXES = ("tz", "tx")


def blend(ema_part, adjusted_part, blend_ratio):
    base = ema_part.astype(jnp.float32)
    return (base + blend_ratio * (adjusted_part.astype(jnp.float32) - base)).astype(jnp.bfloat16)


def convolve(field, kernel, row_padding):
    return lax.conv_general_dilated(
        field[None],
        kernel,
        (1, 1),
        (row_padding, (1, 1)),
        dimension_numbers=("NHCW", "HWOI", "NHCW"),
        preferred_element_type=jnp.float32,
    )[0]


def slot_lookup(tile_ids, slot_row):
    tile_total = slot_row.shape[0]
    matches = tile_ids[:, None] == jnp.arange(tile_total, dtype=jnp.int32)[None, :]
    return jnp.sum(jnp.where(matches, slot_row[None, :], 0), axis=1)


def image_pair(part, image_index, axis):
    other = lax.ppermute(part, "image", [(0, 1), (1, 0)])
    first = jnp.where(image_index == 0, part, other)
    second = jnp.where(image_index == 0, other, part)
    return jnp.concatenate([first, second], axis=axis)


def owner_of(slot, slot_row):
    tiles = jnp.arange(slot_row.shape[0], dtype=jnp.int32)
    return jnp.sum(jnp.where(slot_row == slot, tiles, 0))


def halo_rows(rims, slot_row, my_slot, tz_i, tx_i, n_x):
    column = lax.all_gather(rims, "tz", axis=0, tiled=False)
    received = [None]
    for shift in range(1, n_x):
        dest_tile = tz_i * n_x + (tx_i + shift) % n_x
        dest_slot = lax.dynamic_index_in_dim(slot_row, dest_tile, 0, keepdims=False)
        up_src = owner_of(dest_slot - 1, slot_row)
        down_src = owner_of(dest_slot + 1, slot_row)
        up_part = lax.dynamic_index_in_dim(column, up_src // n_x, 0, keepdims=False)[1]
        down_part = lax.dynamic_index_in_dim(column, down_src // n_x, 0, keepdims=False)[0]
        up_part = jnp.where(up_src % n_x == tx_i, up_part, jnp.zeros_like(up_part))
        down_part = jnp.where(down_src % n_x == tx_i, down_part, jnp.zeros_like(down_part))
        chunk = jnp.stack([up_part, down_part])
        received.append(
            lax.ppermute(chunk, "tx", [(i, (i + shift) % n_x) for i in range(n_x)])
        )
    up_src = owner_of(my_slot - 1, slot_row)
    down_src = owner_of(my_slot + 1, slot_row)
    up_shift = (tx_i - up_src % n_x) % n_x
    down_shift = (tx_i - down_src % n_x) % n_x
    up_own = lax.dynamic_index_in_dim(column, up_src // n_x, 0, keepdims=False)[1]
    down_own = lax.dynamic_index_in_dim(column, down_src // n_x, 0, keepdims=False)[0]
    upper = lax.select_n(up_shift, up_own, *[piece[0] for piece in received[1:]])
    lower = lax.select_n(down_shift, down_own, *[piece[1] for piece in received[1:]])
    return upper, lower


def on_device(
    latent,
    tile_slot,
    tile_count,
    merge_num,
    conv_ema,
    conv_adjusted,
    query_ema,
    query_adjusted,
    kv_ema,
    kv_adjusted,
    out_ema,
    out_adjusted,
    norm_gain,
):
    image_index = lax.axis_index("image")
    tile_index = lax.axis_index("tz") * lax.axis_size("tx") + lax.axis_index("tx")
    slot_row = lax.dynamic_index_in_dim(tile_slot, image_index, 0, keepdims=False)
    live_count = lax.dynamic_index_in_dim(tile_count, image_index, 0, keepdims=False)
    my_slot = lax.dynamic_index_in_dim(slot_row, tile_index, 0, keepdims=False)
    live_flag = (my_slot < live_count).astype(jnp.float32)
    blend_ratio = merge_num[0].astype(jnp.float32) / 16.0

    feats = latent[0]
    tile_rows, chan_shard, tile_cols = feats.shape
    activated = jax.nn.silu(feats.astype(jnp.float32)).astype(jnp.bfloat16)
    rim_rows = jnp.stack([activated[0], activated[-1]])
    n_x = lax.axis_size("tx")
    upper, lower = halo_rows(
        rim_rows, slot_row, my_slot, lax.axis_index("tz"), lax.axis_index("tx"), n_x
    )

    conv_w = image_pair(blend(conv_ema, conv_adjusted, blend_ratio), image_index, 3)
    query_w = image_pair(blend(query_ema, query_adjusted, blend_ratio), image_index, 0)
    kv_w = image_pair(blend(kv_ema, kv_adjusted, blend_ratio), image_index, 0)
    out_w = image_pair(blend(out_ema, out_adjusted, blend_ratio), image_index, 1)
    conv_w = conv_w.reshape(3, 3, -1, conv_w.shape[-1])

    has_upper = my_slot > 0
    has_lower = my_slot + 1 < live_count
    upper = jnp.where(has_upper, upper, jnp.zeros_like(upper))
    lower = jnp.where(has_lower, lower, jnp.zeros_like(lower))
    block_full = lax.all_gather(activated, "tensor", axis=1, tiled=True)
    conv_inner = convolve(block_full, conv_w, (1, 1))
    halo_full = lax.all_gather(jnp.stack([upper, lower]), "tensor", axis=1, tiled=True)
    up_term = convolve(halo_full[0:1], conv_w[0:1], (0, 0))
    down_term = convolve(halo_full[1:2], conv_w[2:3], (0, 0))
    middle = jnp.zeros((tile_rows - 2,) + up_term.shape[1:], jnp.float32)
    conv_out = conv_inner + jnp.concatenate([up_term, middle, down_term], axis=0)
    section_r = lax.reduce_precision(feats.astype(jnp.float32) + conv_out, exponent_bits=8, mantissa_bits=7)
    section = section_r.astype(jnp.bfloat16)
    section_full = lax.all_gather(section, "tensor", axis=1, tiled=True)
    channels = section_full.shape[1]
    cells = tile_rows * tile_cols
    section_f = section_full.astype(jnp.float32)
    rows_f = jnp.transpose(section_f, (0, 2, 1)).reshape(cells, channels)
    root_mean = jnp.sqrt(jnp.mean(rows_f * rows_f, axis=-1) + 1e-06)
    normed = (rows_f * norm_gain.astype(jnp.float32) / root_mean[:, None]).astype(jnp.bfloat16)
    queries = (jnp.dot(normed, query_w, preferred_element_type=jnp.float32) * HD ** (-0.5)).astype(
        jnp.bfloat16
    )
    att_shard = queries.shape[1]
    head_count = att_shard // HD
    pooled = section_r.reshape(
        tile_rows // POOL, POOL, chan_shard, tile_cols // POOL, POOL
    ).mean(axis=(1, 4))
    tok_count = pooled.shape[0] * pooled.shape[2]
    pooled = jnp.transpose(pooled, (0, 2, 1)).astype(jnp.bfloat16).reshape(tok_count, chan_shard)
    pooled = lax.all_gather(pooled, "tensor", axis=1, tiled=True)
    kv_flat = kv_w.reshape(channels, 2 * att_shard)
    kv_local = jnp.dot(pooled, kv_flat, preferred_element_type=jnp.float32).astype(jnp.bfloat16)
    kv_column = lax.all_gather(kv_local, "tz", axis=0, tiled=False)
    kv_all = lax.all_gather(kv_column, "tx", axis=0, tiled=False)
    n_z = kv_all.shape[1]
    kv_rows = kv_all.reshape(-1, 2 * att_shard)
    key_rows = kv_rows[:, :att_shard]
    key_total = key_rows.shape[0]
    key_tile = (
        jnp.arange(n_x, dtype=jnp.int32)[:, None, None]
        + n_x * jnp.arange(n_z, dtype=jnp.int32)[None, :, None]
        + jnp.zeros((1, 1, tok_count), jnp.int32)
    ).reshape(-1)
    key_live = slot_lookup(key_tile, slot_row) < live_count
    key_livef = key_live.astype(jnp.float32)
    key_heads = key_rows.reshape(key_total, head_count, HD)
    value_heads = kv_rows[:, att_shard:].reshape(key_total, head_count, HD)

    total_list, accum_list = [], []
    for head_index in range(head_count):
        scores = lax.dot_general(
            queries[:, head_index * HD:(head_index + 1) * HD],
            key_heads[:, head_index],
            (((1,), (1,)), ((), ())),
            preferred_element_type=jnp.float32,
        )
        scores = jnp.where(key_live[None, :], scores, -1e30)
        top = jnp.max(scores, axis=1)
        expd = jnp.exp(scores - top[:, None]) * key_livef[None, :]
        total_list.append(jnp.sum(expd, axis=1))
        accum_list.append(
            jnp.dot(
                expd.astype(jnp.bfloat16),
                value_heads[:, head_index],
                preferred_element_type=jnp.float32,
            )
        )
    totals = jnp.stack(total_list, axis=1)
    accum = jnp.stack(accum_list, axis=1)
    attended = (accum / totals[..., None]).astype(jnp.bfloat16).reshape(cells, att_shard)
    attended_full = lax.all_gather(attended, "tensor", axis=1, tiled=True)
    projected = lax.dot_general(
        out_w, attended_full, (((1,), (1,)), ((), ())), preferred_element_type=jnp.float32
    )
    projected = jnp.transpose(projected.reshape(chan_shard, tile_rows, tile_cols), (1, 0, 2))
    final = (section_r + projected) * live_flag
    return final.astype(jnp.bfloat16).reshape(1, tile_rows, chan_shard, tile_cols)


def solution(mesh):
    tiles = mesh.shape["tile"]
    inner = 4 if tiles % 4 == 0 else 1
    devices = np.asarray(mesh.devices).reshape(
        (tiles // inner, inner, mesh.shape["image"], mesh.shape["tensor"])
    )
    split = Mesh(devices, ("tz", "tx", "image", "tensor"))
    placed = (
        P("image", TILE_AXES, "tensor", None),
        P(),
        P(),
        P(),
        P(None, None, "tensor", "image", None, None),
        P(None, None, "tensor", "image", None, None),
        P("image", "tensor"),
        P("image", "tensor"),
        P("image", None, "tensor"),
        P("image", None, "tensor"),
        P("tensor", "image"),
        P("tensor", "image"),
        P(),
    )
    return jax.shard_map(
        on_device,
        mesh=split,
        in_specs=placed,
        out_specs=P("image", TILE_AXES, "tensor", None),
        check_vma=False,
    )
```

```python
import numpy as np
import jax
import jax.numpy as jnp
from jax import lax
from jax.sharding import Mesh
from jax.sharding import PartitionSpec as P

HD = 64
POOL = 4
TILE_AXES = ("tz", "tx")


def blend(ema_part, adjusted_part, blend_ratio):
    base = ema_part.astype(jnp.float32)
    return (base + blend_ratio * (adjusted_part.astype(jnp.float32) - base)).astype(jnp.bfloat16)


def convolve(field, kernel, row_padding):
    return lax.conv_general_dilated(
        field[None],
        kernel,
        (1, 1),
        (row_padding, (1, 1)),
        dimension_numbers=("NHCW", "HWOI", "NHCW"),
        preferred_element_type=jnp.float32,
    )[0]


def slot_lookup(tile_ids, slot_row):
    tile_total = slot_row.shape[0]
    matches = tile_ids[:, None] == jnp.arange(tile_total, dtype=jnp.int32)[None, :]
    return jnp.sum(jnp.where(matches, slot_row[None, :], 0), axis=1)


def image_pair(part, image_index, axis):
    other = lax.ppermute(part, "image", [(0, 1), (1, 0)])
    first = jnp.where(image_index == 0, part, other)
    second = jnp.where(image_index == 0, other, part)
    return jnp.concatenate([first, second], axis=axis)


def owner_of(slot, slot_row):
    tiles = jnp.arange(slot_row.shape[0], dtype=jnp.int32)
    return jnp.sum(jnp.where(slot_row == slot, tiles, 0))


def halo_rows(rims, slot_row, my_slot, tz_i, tx_i, n_x):
    column = lax.all_gather(rims, "tz", axis=0, tiled=False)
    chunks = []
    for dest_x in range(n_x):
        dest_tile = tz_i * n_x + dest_x
        dest_slot = lax.dynamic_index_in_dim(slot_row, dest_tile, 0, keepdims=False)
        up_src = owner_of(dest_slot - 1, slot_row)
        down_src = owner_of(dest_slot + 1, slot_row)
        up_part = lax.dynamic_index_in_dim(column, up_src // n_x, 0, keepdims=False)[1]
        down_part = lax.dynamic_index_in_dim(column, down_src // n_x, 0, keepdims=False)[0]
        up_part = jnp.where(up_src % n_x == tx_i, up_part, jnp.zeros_like(up_part))
        down_part = jnp.where(down_src % n_x == tx_i, down_part, jnp.zeros_like(down_part))
        chunks.append(jnp.stack([up_part, down_part]))
    received = lax.all_to_all(jnp.stack(chunks), "tx", 0, 0, tiled=False)
    up_src = owner_of(my_slot - 1, slot_row)
    down_src = owner_of(my_slot + 1, slot_row)
    upper = lax.dynamic_index_in_dim(received, up_src % n_x, 0, keepdims=False)[0]
    lower = lax.dynamic_index_in_dim(received, down_src % n_x, 0, keepdims=False)[1]
    return upper, lower


def on_device(
    latent,
    tile_slot,
    tile_count,
    merge_num,
    conv_ema,
    conv_adjusted,
    query_ema,
    query_adjusted,
    kv_ema,
    kv_adjusted,
    out_ema,
    out_adjusted,
    norm_gain,
):
    image_index = lax.axis_index("image")
    tile_index = lax.axis_index("tz") * lax.axis_size("tx") + lax.axis_index("tx")
    slot_row = lax.dynamic_index_in_dim(tile_slot, image_index, 0, keepdims=False)
    live_count = lax.dynamic_index_in_dim(tile_count, image_index, 0, keepdims=False)
    my_slot = lax.dynamic_index_in_dim(slot_row, tile_index, 0, keepdims=False)
    live_flag = (my_slot < live_count).astype(jnp.float32)
    blend_ratio = merge_num[0].astype(jnp.float32) / 16.0

    feats = latent[0]
    tile_rows, chan_shard, tile_cols = feats.shape
    activated = jax.nn.silu(feats.astype(jnp.float32)).astype(jnp.bfloat16)
    rim_rows = jnp.stack([activated[0], activated[-1]])
    n_x = lax.axis_size("tx")
    upper, lower = halo_rows(
        rim_rows, slot_row, my_slot, lax.axis_index("tz"), lax.axis_index("tx"), n_x
    )

    conv_w = image_pair(blend(conv_ema, conv_adjusted, blend_ratio), image_index, 3)
    query_w = image_pair(blend(query_ema, query_adjusted, blend_ratio), image_index, 0)
    kv_w = image_pair(blend(kv_ema, kv_adjusted, blend_ratio), image_index, 0)
    out_w = image_pair(blend(out_ema, out_adjusted, blend_ratio), image_index, 1)
    conv_w = conv_w.reshape(3, 3, -1, conv_w.shape[-1])

    has_upper = my_slot > 0
    has_lower = my_slot + 1 < live_count
    upper = jnp.where(has_upper, upper, jnp.zeros_like(upper))
    lower = jnp.where(has_lower, lower, jnp.zeros_like(lower))
    block_full = lax.all_gather(activated, "tensor", axis=1, tiled=True)
    conv_inner = convolve(block_full, conv_w, (1, 1))
    halo_full = lax.all_gather(jnp.stack([upper, lower]), "tensor", axis=1, tiled=True)
    up_term = convolve(halo_full[0:1], conv_w[0:1], (0, 0))
    down_term = convolve(halo_full[1:2], conv_w[2:3], (0, 0))
    middle = jnp.zeros((tile_rows - 2,) + up_term.shape[1:], jnp.float32)
    conv_out = conv_inner + jnp.concatenate([up_term, middle, down_term], axis=0)
    section_r = lax.reduce_precision(feats.astype(jnp.float32) + conv_out, exponent_bits=8, mantissa_bits=7)
    section = section_r.astype(jnp.bfloat16)
    section_full = lax.all_gather(section, "tensor", axis=1, tiled=True)
    channels = section_full.shape[1]
    cells = tile_rows * tile_cols
    section_f = section_full.astype(jnp.float32)
    rows_f = jnp.transpose(section_f, (0, 2, 1)).reshape(cells, channels)
    root_mean = jnp.sqrt(jnp.mean(rows_f * rows_f, axis=-1) + 1e-06)
    normed = (rows_f * norm_gain.astype(jnp.float32) / root_mean[:, None]).astype(jnp.bfloat16)
    queries = (jnp.dot(normed, query_w, preferred_element_type=jnp.float32) * HD ** (-0.5)).astype(
        jnp.bfloat16
    )
    att_shard = queries.shape[1]
    head_count = att_shard // HD
    pooled = section_r.reshape(
        tile_rows // POOL, POOL, chan_shard, tile_cols // POOL, POOL
    ).mean(axis=(1, 4))
    tok_count = pooled.shape[0] * pooled.shape[2]
    pooled = jnp.transpose(pooled, (0, 2, 1)).astype(jnp.bfloat16).reshape(tok_count, chan_shard)
    pooled = lax.all_gather(pooled, "tensor", axis=1, tiled=True)
    kv_flat = kv_w.reshape(channels, 2 * att_shard)
    kv_local = jnp.dot(pooled, kv_flat, preferred_element_type=jnp.float32).astype(jnp.bfloat16)
    kv_column = lax.all_gather(kv_local, "tz", axis=0, tiled=False)
    kv_all = lax.all_gather(kv_column, "tx", axis=0, tiled=False)
    n_z = kv_all.shape[1]
    kv_rows = kv_all.reshape(-1, 2 * att_shard)
    key_rows = kv_rows[:, :att_shard]
    key_total = key_rows.shape[0]
    key_tile = (
        jnp.arange(n_x, dtype=jnp.int32)[:, None, None]
        + n_x * jnp.arange(n_z, dtype=jnp.int32)[None, :, None]
        + jnp.zeros((1, 1, tok_count), jnp.int32)
    ).reshape(-1)
    key_live = slot_lookup(key_tile, slot_row) < live_count
    key_livef = key_live.astype(jnp.float32)
    key_heads = key_rows.reshape(key_total, head_count, HD)
    value_heads = kv_rows[:, att_shard:].reshape(key_total, head_count, HD)

    total_list, accum_list = [], []
    for head_index in range(head_count):
        scores = lax.dot_general(
            queries[:, head_index * HD:(head_index + 1) * HD],
            key_heads[:, head_index],
            (((1,), (1,)), ((), ())),
            preferred_element_type=jnp.float32,
        )
        scores = jnp.where(key_live[None, :], scores, -1e30)
        top = jnp.max(scores, axis=1)
        expd = jnp.exp(scores - top[:, None]) * key_livef[None, :]
        total_list.append(jnp.sum(expd, axis=1))
        accum_list.append(
            jnp.dot(
                expd.astype(jnp.bfloat16),
                value_heads[:, head_index],
                preferred_element_type=jnp.float32,
            )
        )
    totals = jnp.stack(total_list, axis=1)
    accum = jnp.stack(accum_list, axis=1)
    attended = (accum / totals[..., None]).astype(jnp.bfloat16).reshape(cells, att_shard)
    attended_full = lax.all_gather(attended, "tensor", axis=1, tiled=True)
    projected = lax.dot_general(
        out_w, attended_full, (((1,), (1,)), ((), ())), preferred_element_type=jnp.float32
    )
    projected = jnp.transpose(projected.reshape(chan_shard, tile_rows, tile_cols), (1, 0, 2))
    final = (section_r + projected) * live_flag
    return final.astype(jnp.bfloat16).reshape(1, tile_rows, chan_shard, tile_cols)


def solution(mesh):
    tiles = mesh.shape["tile"]
    inner = 4 if tiles % 4 == 0 else 1
    devices = np.asarray(mesh.devices).reshape(
        (tiles // inner, inner, mesh.shape["image"], mesh.shape["tensor"])
    )
    split = Mesh(devices, ("tz", "tx", "image", "tensor"))
    placed = (
        P("image", TILE_AXES, "tensor", None),
        P(),
        P(),
        P(),
        P(None, None, "tensor", "image", None, None),
        P(None, None, "tensor", "image", None, None),
        P("image", "tensor"),
        P("image", "tensor"),
        P("image", None, "tensor"),
        P("image", None, "tensor"),
        P("tensor", "image"),
        P("tensor", "image"),
        P(),
    )
    return jax.shard_map(
        on_device,
        mesh=split,
        in_specs=placed,
        out_specs=P("image", TILE_AXES, "tensor", None),
        check_vma=False,
    )
```

```python
import numpy as np
import jax
import jax.numpy as jnp
from jax import lax
from jax.sharding import Mesh
from jax.sharding import PartitionSpec as P

HD = 64
POOL = 4
TILE_AXES = ("tz", "tx")


def blend(ema_part, adjusted_part, blend_ratio):
    base = ema_part.astype(jnp.float32)
    return (base + blend_ratio * (adjusted_part.astype(jnp.float32) - base)).astype(jnp.bfloat16)


def convolve(field, kernel, row_padding):
    return lax.conv_general_dilated(
        field[None],
        kernel,
        (1, 1),
        (row_padding, (1, 1)),
        dimension_numbers=("NHCW", "HWOI", "NHCW"),
        preferred_element_type=jnp.float32,
    )[0]


def slot_lookup(tile_ids, slot_row):
    tile_total = slot_row.shape[0]
    matches = tile_ids[:, None] == jnp.arange(tile_total, dtype=jnp.int32)[None, :]
    return jnp.sum(jnp.where(matches, slot_row[None, :], 0), axis=1)


def image_pair(part, image_index, axis):
    other = lax.ppermute(part, "image", [(0, 1), (1, 0)])
    first = jnp.where(image_index == 0, part, other)
    second = jnp.where(image_index == 0, other, part)
    return jnp.concatenate([first, second], axis=axis)


def owner_of(slot, slot_row):
    tiles = jnp.arange(slot_row.shape[0], dtype=jnp.int32)
    return jnp.sum(jnp.where(slot_row == slot, tiles, 0))


def halo_rows(rims, early, slot_row, my_slot, tz_i, tx_i, n_x):
    column = lax.all_gather(rims, "tz", axis=0, tiled=False)
    column, early = lax.optimization_barrier((column, early))
    chunks = []
    for dest_x in range(n_x):
        dest_tile = tz_i * n_x + dest_x
        dest_slot = lax.dynamic_index_in_dim(slot_row, dest_tile, 0, keepdims=False)
        up_src = owner_of(dest_slot - 1, slot_row)
        down_src = owner_of(dest_slot + 1, slot_row)
        up_part = lax.dynamic_index_in_dim(column, up_src // n_x, 0, keepdims=False)[1]
        down_part = lax.dynamic_index_in_dim(column, down_src // n_x, 0, keepdims=False)[0]
        up_part = jnp.where(up_src % n_x == tx_i, up_part, jnp.zeros_like(up_part))
        down_part = jnp.where(down_src % n_x == tx_i, down_part, jnp.zeros_like(down_part))
        chunks.append(jnp.stack([up_part, down_part]))
    received = lax.all_to_all(jnp.stack(chunks), "tx", 0, 0, tiled=False)
    up_src = owner_of(my_slot - 1, slot_row)
    down_src = owner_of(my_slot + 1, slot_row)
    upper = lax.dynamic_index_in_dim(received, up_src % n_x, 0, keepdims=False)[0]
    lower = lax.dynamic_index_in_dim(received, down_src % n_x, 0, keepdims=False)[1]
    return upper, lower, early


def on_device(
    latent,
    tile_slot,
    tile_count,
    merge_num,
    conv_ema,
    conv_adjusted,
    query_ema,
    query_adjusted,
    kv_ema,
    kv_adjusted,
    out_ema,
    out_adjusted,
    norm_gain,
):
    image_index = lax.axis_index("image")
    tile_index = lax.axis_index("tz") * lax.axis_size("tx") + lax.axis_index("tx")
    slot_row = lax.dynamic_index_in_dim(tile_slot, image_index, 0, keepdims=False)
    live_count = lax.dynamic_index_in_dim(tile_count, image_index, 0, keepdims=False)
    my_slot = lax.dynamic_index_in_dim(slot_row, tile_index, 0, keepdims=False)
    live_flag = (my_slot < live_count).astype(jnp.float32)
    blend_ratio = merge_num[0].astype(jnp.float32) / 16.0

    feats = latent[0]
    tile_rows, chan_shard, tile_cols = feats.shape
    activated = jax.nn.silu(feats.astype(jnp.float32)).astype(jnp.bfloat16)
    rim_rows = jnp.stack([activated[0], activated[-1]])
    n_x = lax.axis_size("tx")
    conv_w = image_pair(blend(conv_ema, conv_adjusted, blend_ratio), image_index, 3)
    query_w = image_pair(blend(query_ema, query_adjusted, blend_ratio), image_index, 0)
    kv_w = image_pair(blend(kv_ema, kv_adjusted, blend_ratio), image_index, 0)
    out_w = image_pair(blend(out_ema, out_adjusted, blend_ratio), image_index, 1)
    conv_w = conv_w.reshape(3, 3, -1, conv_w.shape[-1])

    block_full = lax.all_gather(activated, "tensor", axis=1, tiled=True)
    conv_inner = convolve(block_full, conv_w, (1, 1))
    upper, lower, conv_inner = halo_rows(
        rim_rows, conv_inner, slot_row, my_slot, lax.axis_index("tz"), lax.axis_index("tx"), n_x
    )

    has_upper = my_slot > 0
    has_lower = my_slot + 1 < live_count
    upper = jnp.where(has_upper, upper, jnp.zeros_like(upper))
    lower = jnp.where(has_lower, lower, jnp.zeros_like(lower))
    halo_full = lax.all_gather(jnp.stack([upper, lower]), "tensor", axis=1, tiled=True)
    up_term = convolve(halo_full[0:1], conv_w[0:1], (0, 0))
    down_term = convolve(halo_full[1:2], conv_w[2:3], (0, 0))
    middle = jnp.zeros((tile_rows - 2,) + up_term.shape[1:], jnp.float32)
    conv_out = conv_inner + jnp.concatenate([up_term, middle, down_term], axis=0)
    section_r = lax.reduce_precision(feats.astype(jnp.float32) + conv_out, exponent_bits=8, mantissa_bits=7)
    section = section_r.astype(jnp.bfloat16)
    section_full = lax.all_gather(section, "tensor", axis=1, tiled=True)
    channels = section_full.shape[1]
    cells = tile_rows * tile_cols
    section_f = section_full.astype(jnp.float32)
    rows_f = jnp.transpose(section_f, (0, 2, 1)).reshape(cells, channels)
    root_mean = jnp.sqrt(jnp.mean(rows_f * rows_f, axis=-1) + 1e-06)
    normed = (rows_f * norm_gain.astype(jnp.float32) / root_mean[:, None]).astype(jnp.bfloat16)
    queries = (jnp.dot(normed, query_w, preferred_element_type=jnp.float32) * HD ** (-0.5)).astype(
        jnp.bfloat16
    )
    att_shard = queries.shape[1]
    head_count = att_shard // HD
    pooled = section_r.reshape(
        tile_rows // POOL, POOL, chan_shard, tile_cols // POOL, POOL
    ).mean(axis=(1, 4))
    tok_count = pooled.shape[0] * pooled.shape[2]
    pooled = jnp.transpose(pooled, (0, 2, 1)).astype(jnp.bfloat16).reshape(tok_count, chan_shard)
    pooled = lax.all_gather(pooled, "tensor", axis=1, tiled=True)
    kv_flat = kv_w.reshape(channels, 2 * att_shard)
    kv_local = jnp.dot(pooled, kv_flat, preferred_element_type=jnp.float32).astype(jnp.bfloat16)
    kv_column = lax.all_gather(kv_local, "tz", axis=0, tiled=False)
    kv_all = lax.all_gather(kv_column, "tx", axis=0, tiled=False)
    n_z = kv_all.shape[1]
    kv_rows = kv_all.reshape(-1, 2 * att_shard)
    key_rows = kv_rows[:, :att_shard]
    key_total = key_rows.shape[0]
    key_tile = (
        jnp.arange(n_x, dtype=jnp.int32)[:, None, None]
        + n_x * jnp.arange(n_z, dtype=jnp.int32)[None, :, None]
        + jnp.zeros((1, 1, tok_count), jnp.int32)
    ).reshape(-1)
    key_live = slot_lookup(key_tile, slot_row) < live_count
    key_livef = key_live.astype(jnp.float32)
    key_heads = key_rows.reshape(key_total, head_count, HD)
    value_heads = kv_rows[:, att_shard:].reshape(key_total, head_count, HD)

    total_list, accum_list = [], []
    for head_index in range(head_count):
        scores = lax.dot_general(
            queries[:, head_index * HD:(head_index + 1) * HD],
            key_heads[:, head_index],
            (((1,), (1,)), ((), ())),
            preferred_element_type=jnp.float32,
        )
        scores = jnp.where(key_live[None, :], scores, -1e30)
        top = jnp.max(scores, axis=1)
        expd = jnp.exp(scores - top[:, None]) * key_livef[None, :]
        total_list.append(jnp.sum(expd, axis=1))
        accum_list.append(
            jnp.dot(
                expd.astype(jnp.bfloat16),
                value_heads[:, head_index],
                preferred_element_type=jnp.float32,
            )
        )
    totals = jnp.stack(total_list, axis=1)
    accum = jnp.stack(accum_list, axis=1)
    attended = (accum / totals[..., None]).astype(jnp.bfloat16).reshape(cells, att_shard)
    attended_full = lax.all_gather(attended, "tensor", axis=1, tiled=True)
    projected = lax.dot_general(
        out_w, attended_full, (((1,), (1,)), ((), ())), preferred_element_type=jnp.float32
    )
    projected = jnp.transpose(projected.reshape(chan_shard, tile_rows, tile_cols), (1, 0, 2))
    final = (section_r + projected) * live_flag
    return final.astype(jnp.bfloat16).reshape(1, tile_rows, chan_shard, tile_cols)


def solution(mesh):
    tiles = mesh.shape["tile"]
    inner = 4 if tiles % 4 == 0 else 1
    devices = np.asarray(mesh.devices).reshape(
        (tiles // inner, inner, mesh.shape["image"], mesh.shape["tensor"])
    )
    split = Mesh(devices, ("tz", "tx", "image", "tensor"))
    placed = (
        P("image", TILE_AXES, "tensor", None),
        P(),
        P(),
        P(),
        P(None, None, "tensor", "image", None, None),
        P(None, None, "tensor", "image", None, None),
        P("image", "tensor"),
        P("image", "tensor"),
        P("image", None, "tensor"),
        P("image", None, "tensor"),
        P("tensor", "image"),
        P("tensor", "image"),
        P(),
    )
    return jax.shard_map(
        on_device,
        mesh=split,
        in_specs=placed,
        out_specs=P("image", TILE_AXES, "tensor", None),
        check_vma=False,
    )
```

```python
import numpy as np
import jax
import jax.numpy as jnp
from jax import lax
from jax.sharding import Mesh
from jax.sharding import PartitionSpec as P

HD = 64
POOL = 4
TILE_AXES = ("tz", "tx")


def blend(ema_part, adjusted_part, blend_ratio):
    base = ema_part.astype(jnp.float32)
    return (base + blend_ratio * (adjusted_part.astype(jnp.float32) - base)).astype(jnp.bfloat16)


def convolve(field, kernel, row_padding):
    return lax.conv_general_dilated(
        field[None],
        kernel,
        (1, 1),
        (row_padding, (1, 1)),
        dimension_numbers=("NHCW", "HWOI", "NHCW"),
        preferred_element_type=jnp.float32,
    )[0]


def slot_lookup(tile_ids, slot_row):
    tile_total = slot_row.shape[0]
    matches = tile_ids[:, None] == jnp.arange(tile_total, dtype=jnp.int32)[None, :]
    return jnp.sum(jnp.where(matches, slot_row[None, :], 0), axis=1)


def image_pair(part, image_index, axis):
    other = lax.ppermute(part, "image", [(0, 1), (1, 0)])
    first = jnp.where(image_index == 0, part, other)
    second = jnp.where(image_index == 0, other, part)
    return jnp.concatenate([first, second], axis=axis)


def owner_of(slot, slot_row):
    tiles = jnp.arange(slot_row.shape[0], dtype=jnp.int32)
    return jnp.sum(jnp.where(slot_row == slot, tiles, 0))


def halo_rows(rims, slot_row, my_slot, tz_i, tx_i, n_x):
    column = lax.all_gather(rims, "tz", axis=0, tiled=False)
    received = [None]
    for shift in range(1, n_x):
        dest_tile = tz_i * n_x + (tx_i + shift) % n_x
        dest_slot = lax.dynamic_index_in_dim(slot_row, dest_tile, 0, keepdims=False)
        up_src = owner_of(dest_slot - 1, slot_row)
        down_src = owner_of(dest_slot + 1, slot_row)
        up_part = lax.dynamic_index_in_dim(column, up_src // n_x, 0, keepdims=False)[1]
        down_part = lax.dynamic_index_in_dim(column, down_src // n_x, 0, keepdims=False)[0]
        up_part = jnp.where(up_src % n_x == tx_i, up_part, jnp.zeros_like(up_part))
        down_part = jnp.where(down_src % n_x == tx_i, down_part, jnp.zeros_like(down_part))
        chunk = jnp.stack([up_part, down_part])
        received.append(
            lax.ppermute(chunk, "tx", [(i, (i + shift) % n_x) for i in range(n_x)])
        )
    up_src = owner_of(my_slot - 1, slot_row)
    down_src = owner_of(my_slot + 1, slot_row)
    up_shift = (tx_i - up_src % n_x) % n_x
    down_shift = (tx_i - down_src % n_x) % n_x
    up_own = lax.dynamic_index_in_dim(column, up_src // n_x, 0, keepdims=False)[1]
    down_own = lax.dynamic_index_in_dim(column, down_src // n_x, 0, keepdims=False)[0]
    upper = lax.select_n(up_shift, up_own, *[piece[0] for piece in received[1:]])
    lower = lax.select_n(down_shift, down_own, *[piece[1] for piece in received[1:]])
    return upper, lower


def on_device(
    latent,
    tile_slot,
    tile_count,
    merge_num,
    conv_ema,
    conv_adjusted,
    query_ema,
    query_adjusted,
    kv_ema,
    kv_adjusted,
    out_ema,
    out_adjusted,
    norm_gain,
):
    image_index = lax.axis_index("image")
    tile_index = lax.axis_index("tz") * lax.axis_size("tx") + lax.axis_index("tx")
    slot_row = lax.dynamic_index_in_dim(tile_slot, image_index, 0, keepdims=False)
    live_count = lax.dynamic_index_in_dim(tile_count, image_index, 0, keepdims=False)
    my_slot = lax.dynamic_index_in_dim(slot_row, tile_index, 0, keepdims=False)
    live_flag = (my_slot < live_count).astype(jnp.float32)
    blend_ratio = merge_num[0].astype(jnp.float32) / 16.0

    feats = latent[0]
    tile_rows, chan_shard, tile_cols = feats.shape
    activated = jax.nn.silu(feats.astype(jnp.float32)).astype(jnp.bfloat16)
    rim_rows = jnp.stack([feats[0], feats[-1]])
    n_x = lax.axis_size("tx")
    upper, lower = halo_rows(
        rim_rows, slot_row, my_slot, lax.axis_index("tz"), lax.axis_index("tx"), n_x
    )

    conv_w = image_pair(blend(conv_ema, conv_adjusted, blend_ratio), image_index, 3)
    query_w = image_pair(blend(query_ema, query_adjusted, blend_ratio), image_index, 0)
    kv_w = image_pair(blend(kv_ema, kv_adjusted, blend_ratio), image_index, 0)
    out_w = image_pair(blend(out_ema, out_adjusted, blend_ratio), image_index, 1)
    conv_w = conv_w.reshape(3, 3, -1, conv_w.shape[-1])

    has_upper = my_slot > 0
    has_lower = my_slot + 1 < live_count
    upper = jax.nn.silu(upper.astype(jnp.float32)).astype(jnp.bfloat16)
    lower = jax.nn.silu(lower.astype(jnp.float32)).astype(jnp.bfloat16)
    upper = jnp.where(has_upper, upper, jnp.zeros_like(upper))
    lower = jnp.where(has_lower, lower, jnp.zeros_like(lower))
    block_full = lax.all_gather(activated, "tensor", axis=1, tiled=True)
    conv_inner = convolve(block_full, conv_w, (1, 1))
    halo_full = lax.all_gather(jnp.stack([upper, lower]), "tensor", axis=1, tiled=True)
    up_term = convolve(halo_full[0:1], conv_w[0:1], (0, 0))
    down_term = convolve(halo_full[1:2], conv_w[2:3], (0, 0))
    middle = jnp.zeros((tile_rows - 2,) + up_term.shape[1:], jnp.float32)
    conv_out = conv_inner + jnp.concatenate([up_term, middle, down_term], axis=0)
    section_r = lax.reduce_precision(feats.astype(jnp.float32) + conv_out, exponent_bits=8, mantissa_bits=7)
    section = section_r.astype(jnp.bfloat16)
    section_full = lax.all_gather(section, "tensor", axis=1, tiled=True)
    channels = section_full.shape[1]
    cells = tile_rows * tile_cols
    section_f = section_full.astype(jnp.float32)
    rows_f = jnp.transpose(section_f, (0, 2, 1)).reshape(cells, channels)
    root_mean = jnp.sqrt(jnp.mean(rows_f * rows_f, axis=-1) + 1e-06)
    normed = (rows_f * norm_gain.astype(jnp.float32) / root_mean[:, None]).astype(jnp.bfloat16)
    queries = (jnp.dot(normed, query_w, preferred_element_type=jnp.float32) * HD ** (-0.5)).astype(
        jnp.bfloat16
    )
    att_shard = queries.shape[1]
    head_count = att_shard // HD
    pooled = section_r.reshape(
        tile_rows // POOL, POOL, chan_shard, tile_cols // POOL, POOL
    ).mean(axis=(1, 4))
    tok_count = pooled.shape[0] * pooled.shape[2]
    pooled = jnp.transpose(pooled, (0, 2, 1)).astype(jnp.bfloat16).reshape(tok_count, chan_shard)
    pooled = lax.all_gather(pooled, "tensor", axis=1, tiled=True)
    kv_flat = kv_w.reshape(channels, 2 * att_shard)
    kv_local = jnp.dot(pooled, kv_flat, preferred_element_type=jnp.float32).astype(jnp.bfloat16)
    kv_column = lax.all_gather(kv_local, "tz", axis=0, tiled=False)
    kv_all = lax.all_gather(kv_column, "tx", axis=0, tiled=False)
    n_z = kv_all.shape[1]
    kv_rows = kv_all.reshape(-1, 2 * att_shard)
    key_rows = kv_rows[:, :att_shard]
    key_total = key_rows.shape[0]
    key_tile = (
        jnp.arange(n_x, dtype=jnp.int32)[:, None, None]
        + n_x * jnp.arange(n_z, dtype=jnp.int32)[None, :, None]
        + jnp.zeros((1, 1, tok_count), jnp.int32)
    ).reshape(-1)
    key_live = slot_lookup(key_tile, slot_row) < live_count
    key_livef = key_live.astype(jnp.float32)
    key_heads = key_rows.reshape(key_total, head_count, HD)
    value_heads = kv_rows[:, att_shard:].reshape(key_total, head_count, HD)

    total_list, accum_list = [], []
    for head_index in range(head_count):
        scores = lax.dot_general(
            queries[:, head_index * HD:(head_index + 1) * HD],
            key_heads[:, head_index],
            (((1,), (1,)), ((), ())),
            preferred_element_type=jnp.float32,
        )
        scores = jnp.where(key_live[None, :], scores, -1e30)
        top = jnp.max(scores, axis=1)
        expd = jnp.exp(scores - top[:, None]) * key_livef[None, :]
        total_list.append(jnp.sum(expd, axis=1))
        accum_list.append(
            jnp.dot(
                expd.astype(jnp.bfloat16),
                value_heads[:, head_index],
                preferred_element_type=jnp.float32,
            )
        )
    totals = jnp.stack(total_list, axis=1)
    accum = jnp.stack(accum_list, axis=1)
    attended = (accum / totals[..., None]).astype(jnp.bfloat16).reshape(cells, att_shard)
    attended_full = lax.all_gather(attended, "tensor", axis=1, tiled=True)
    projected = lax.dot_general(
        out_w, attended_full, (((1,), (1,)), ((), ())), preferred_element_type=jnp.float32
    )
    projected = jnp.transpose(projected.reshape(chan_shard, tile_rows, tile_cols), (1, 0, 2))
    final = (section_r + projected) * live_flag
    return final.astype(jnp.bfloat16).reshape(1, tile_rows, chan_shard, tile_cols)


def solution(mesh):
    tiles = mesh.shape["tile"]
    inner = 4 if tiles % 4 == 0 else 1
    devices = np.asarray(mesh.devices).reshape(
        (tiles // inner, inner, mesh.shape["image"], mesh.shape["tensor"])
    )
    split = Mesh(devices, ("tz", "tx", "image", "tensor"))
    placed = (
        P("image", TILE_AXES, "tensor", None),
        P(),
        P(),
        P(),
        P(None, None, "tensor", "image", None, None),
        P(None, None, "tensor", "image", None, None),
        P("image", "tensor"),
        P("image", "tensor"),
        P("image", None, "tensor"),
        P("image", None, "tensor"),
        P("tensor", "image"),
        P("tensor", "image"),
        P(),
    )
    return jax.shard_map(
        on_device,
        mesh=split,
        in_specs=placed,
        out_specs=P("image", TILE_AXES, "tensor", None),
        check_vma=False,
    )
```

```python
import numpy as np
import jax
import jax.numpy as jnp
from jax import lax
from jax.sharding import Mesh
from jax.sharding import PartitionSpec as P

HD = 64
POOL = 4
TILE_AXES = ("tz", "tx")


def blend(ema_part, adjusted_part, blend_ratio):
    base = ema_part.astype(jnp.float32)
    return (base + blend_ratio * (adjusted_part.astype(jnp.float32) - base)).astype(jnp.bfloat16)


def convolve(field, kernel, row_padding):
    return lax.conv_general_dilated(
        field[None],
        kernel,
        (1, 1),
        (row_padding, (1, 1)),
        dimension_numbers=("NHCW", "HWOI", "NHCW"),
        preferred_element_type=jnp.float32,
    )[0]


def slot_lookup(tile_ids, slot_row):
    tile_total = slot_row.shape[0]
    matches = tile_ids[:, None] == jnp.arange(tile_total, dtype=jnp.int32)[None, :]
    return jnp.sum(jnp.where(matches, slot_row[None, :], 0), axis=1)


def image_pair(part, image_index, axis):
    other = lax.ppermute(part, "image", [(0, 1), (1, 0)])
    first = jnp.where(image_index == 0, part, other)
    second = jnp.where(image_index == 0, other, part)
    return jnp.concatenate([first, second], axis=axis)


def owner_of(slot, slot_row):
    tiles = jnp.arange(slot_row.shape[0], dtype=jnp.int32)
    return jnp.sum(jnp.where(slot_row == slot, tiles, 0))


def halo_rows(rims, slot_row, my_slot, tz_i, tx_i, n_x):
    column = lax.all_gather(rims, "tz", axis=0, tiled=False)
    received = [None]
    for shift in range(1, n_x):
        dest_tile = tz_i * n_x + (tx_i + shift) % n_x
        dest_slot = lax.dynamic_index_in_dim(slot_row, dest_tile, 0, keepdims=False)
        up_src = owner_of(dest_slot - 1, slot_row)
        down_src = owner_of(dest_slot + 1, slot_row)
        up_part = lax.dynamic_index_in_dim(column, up_src // n_x, 0, keepdims=False)[1]
        down_part = lax.dynamic_index_in_dim(column, down_src // n_x, 0, keepdims=False)[0]
        up_part = jnp.where(up_src % n_x == tx_i, up_part, jnp.zeros_like(up_part))
        down_part = jnp.where(down_src % n_x == tx_i, down_part, jnp.zeros_like(down_part))
        received.append(jnp.stack([up_part, down_part]))
    sent = lax.all_gather(jnp.stack(received[1:]), "tx", axis=0, tiled=False)
    received = [None] + [
        lax.dynamic_index_in_dim(sent, (tx_i - shift) % n_x, 0, keepdims=False)[shift - 1]
        for shift in range(1, n_x)
    ]
    up_src = owner_of(my_slot - 1, slot_row)
    down_src = owner_of(my_slot + 1, slot_row)
    up_shift = (tx_i - up_src % n_x) % n_x
    down_shift = (tx_i - down_src % n_x) % n_x
    up_own = lax.dynamic_index_in_dim(column, up_src // n_x, 0, keepdims=False)[1]
    down_own = lax.dynamic_index_in_dim(column, down_src // n_x, 0, keepdims=False)[0]
    upper = lax.select_n(up_shift, up_own, *[piece[0] for piece in received[1:]])
    lower = lax.select_n(down_shift, down_own, *[piece[1] for piece in received[1:]])
    return upper, lower


def on_device(
    latent,
    tile_slot,
    tile_count,
    merge_num,
    conv_ema,
    conv_adjusted,
    query_ema,
    query_adjusted,
    kv_ema,
    kv_adjusted,
    out_ema,
    out_adjusted,
    norm_gain,
):
    image_index = lax.axis_index("image")
    tile_index = lax.axis_index("tz") * lax.axis_size("tx") + lax.axis_index("tx")
    slot_row = lax.dynamic_index_in_dim(tile_slot, image_index, 0, keepdims=False)
    live_count = lax.dynamic_index_in_dim(tile_count, image_index, 0, keepdims=False)
    my_slot = lax.dynamic_index_in_dim(slot_row, tile_index, 0, keepdims=False)
    live_flag = (my_slot < live_count).astype(jnp.float32)
    blend_ratio = merge_num[0].astype(jnp.float32) / 16.0

    feats = latent[0]
    tile_rows, chan_shard, tile_cols = feats.shape
    activated = jax.nn.silu(feats.astype(jnp.float32)).astype(jnp.bfloat16)
    rim_rows = jnp.stack([feats[0], feats[-1]])
    n_x = lax.axis_size("tx")
    upper, lower = halo_rows(
        rim_rows, slot_row, my_slot, lax.axis_index("tz"), lax.axis_index("tx"), n_x
    )

    conv_w = image_pair(blend(conv_ema, conv_adjusted, blend_ratio), image_index, 3)
    query_w = image_pair(blend(query_ema, query_adjusted, blend_ratio), image_index, 0)
    kv_w = image_pair(blend(kv_ema, kv_adjusted, blend_ratio), image_index, 0)
    out_w = image_pair(blend(out_ema, out_adjusted, blend_ratio), image_index, 1)
    conv_w = conv_w.reshape(3, 3, -1, conv_w.shape[-1])

    has_upper = my_slot > 0
    has_lower = my_slot + 1 < live_count
    upper = jax.nn.silu(upper.astype(jnp.float32)).astype(jnp.bfloat16)
    lower = jax.nn.silu(lower.astype(jnp.float32)).astype(jnp.bfloat16)
    upper = jnp.where(has_upper, upper, jnp.zeros_like(upper))
    lower = jnp.where(has_lower, lower, jnp.zeros_like(lower))
    block_full = lax.all_gather(activated, "tensor", axis=1, tiled=True)
    conv_inner = convolve(block_full, conv_w, (1, 1))
    halo_full = lax.all_gather(jnp.stack([upper, lower]), "tensor", axis=1, tiled=True)
    up_term = convolve(halo_full[0:1], conv_w[0:1], (0, 0))
    down_term = convolve(halo_full[1:2], conv_w[2:3], (0, 0))
    middle = jnp.zeros((tile_rows - 2,) + up_term.shape[1:], jnp.float32)
    conv_out = conv_inner + jnp.concatenate([up_term, middle, down_term], axis=0)
    section_r = lax.reduce_precision(feats.astype(jnp.float32) + conv_out, exponent_bits=8, mantissa_bits=7)
    section = section_r.astype(jnp.bfloat16)
    section_full = lax.all_gather(section, "tensor", axis=1, tiled=True)
    channels = section_full.shape[1]
    cells = tile_rows * tile_cols
    section_f = section_full.astype(jnp.float32)
    rows_f = jnp.transpose(section_f, (0, 2, 1)).reshape(cells, channels)
    root_mean = jnp.sqrt(jnp.mean(rows_f * rows_f, axis=-1) + 1e-06)
    normed = (rows_f * norm_gain.astype(jnp.float32) / root_mean[:, None]).astype(jnp.bfloat16)
    queries = (jnp.dot(normed, query_w, preferred_element_type=jnp.float32) * HD ** (-0.5)).astype(
        jnp.bfloat16
    )
    att_shard = queries.shape[1]
    head_count = att_shard // HD
    pooled = section_r.reshape(
        tile_rows // POOL, POOL, chan_shard, tile_cols // POOL, POOL
    ).mean(axis=(1, 4))
    tok_count = pooled.shape[0] * pooled.shape[2]
    pooled = jnp.transpose(pooled, (0, 2, 1)).astype(jnp.bfloat16).reshape(tok_count, chan_shard)
    pooled = lax.all_gather(pooled, "tensor", axis=1, tiled=True)
    kv_flat = kv_w.reshape(channels, 2 * att_shard)
    kv_local = jnp.dot(pooled, kv_flat, preferred_element_type=jnp.float32).astype(jnp.bfloat16)
    kv_column = lax.all_gather(kv_local, "tz", axis=0, tiled=False)
    kv_all = lax.all_gather(kv_column, "tx", axis=0, tiled=False)
    n_z = kv_all.shape[1]
    kv_rows = kv_all.reshape(-1, 2 * att_shard)
    key_rows = kv_rows[:, :att_shard]
    key_total = key_rows.shape[0]
    key_tile = (
        jnp.arange(n_x, dtype=jnp.int32)[:, None, None]
        + n_x * jnp.arange(n_z, dtype=jnp.int32)[None, :, None]
        + jnp.zeros((1, 1, tok_count), jnp.int32)
    ).reshape(-1)
    key_live = slot_lookup(key_tile, slot_row) < live_count
    key_livef = key_live.astype(jnp.float32)
    key_heads = key_rows.reshape(key_total, head_count, HD)
    value_heads = kv_rows[:, att_shard:].reshape(key_total, head_count, HD)

    total_list, accum_list = [], []
    for head_index in range(head_count):
        scores = lax.dot_general(
            queries[:, head_index * HD:(head_index + 1) * HD],
            key_heads[:, head_index],
            (((1,), (1,)), ((), ())),
            preferred_element_type=jnp.float32,
        )
        scores = jnp.where(key_live[None, :], scores, -1e30)
        top = jnp.max(scores, axis=1)
        expd = jnp.exp(scores - top[:, None]) * key_livef[None, :]
        total_list.append(jnp.sum(expd, axis=1))
        accum_list.append(
            jnp.dot(
                expd.astype(jnp.bfloat16),
                value_heads[:, head_index],
                preferred_element_type=jnp.float32,
            )
        )
    totals = jnp.stack(total_list, axis=1)
    accum = jnp.stack(accum_list, axis=1)
    attended = (accum / totals[..., None]).astype(jnp.bfloat16).reshape(cells, att_shard)
    attended_full = lax.all_gather(attended, "tensor", axis=1, tiled=True)
    projected = lax.dot_general(
        out_w, attended_full, (((1,), (1,)), ((), ())), preferred_element_type=jnp.float32
    )
    projected = jnp.transpose(projected.reshape(chan_shard, tile_rows, tile_cols), (1, 0, 2))
    final = (section_r + projected) * live_flag
    return final.astype(jnp.bfloat16).reshape(1, tile_rows, chan_shard, tile_cols)


def solution(mesh):
    tiles = mesh.shape["tile"]
    inner = 4 if tiles % 4 == 0 else 1
    devices = np.asarray(mesh.devices).reshape(
        (tiles // inner, inner, mesh.shape["image"], mesh.shape["tensor"])
    )
    split = Mesh(devices, ("tz", "tx", "image", "tensor"))
    placed = (
        P("image", TILE_AXES, "tensor", None),
        P(),
        P(),
        P(),
        P(None, None, "tensor", "image", None, None),
        P(None, None, "tensor", "image", None, None),
        P("image", "tensor"),
        P("image", "tensor"),
        P("image", None, "tensor"),
        P("image", None, "tensor"),
        P("tensor", "image"),
        P("tensor", "image"),
        P(),
    )
    return jax.shard_map(
        on_device,
        mesh=split,
        in_specs=placed,
        out_specs=P("image", TILE_AXES, "tensor", None),
        check_vma=False,
    )
```

```python
import numpy as np
import jax
import jax.numpy as jnp
from jax import lax
from jax.sharding import Mesh
from jax.sharding import PartitionSpec as P

HD = 64
POOL = 4
TILE_AXES = ("tz", "tx")


def blend(ema_part, adjusted_part, blend_ratio):
    base = ema_part.astype(jnp.float32)
    return (base + blend_ratio * (adjusted_part.astype(jnp.float32) - base)).astype(jnp.bfloat16)


def convolve(field, kernel, row_padding):
    return lax.conv_general_dilated(
        field[None],
        kernel,
        (1, 1),
        (row_padding, (1, 1)),
        dimension_numbers=("NHCW", "HWOI", "NHCW"),
        preferred_element_type=jnp.float32,
    )[0]


def slot_lookup(tile_ids, slot_row):
    tile_total = slot_row.shape[0]
    matches = tile_ids[:, None] == jnp.arange(tile_total, dtype=jnp.int32)[None, :]
    return jnp.sum(jnp.where(matches, slot_row[None, :], 0), axis=1)


def image_pair(part, image_index, axis):
    other = lax.ppermute(part, "image", [(0, 1), (1, 0)])
    first = jnp.where(image_index == 0, part, other)
    second = jnp.where(image_index == 0, other, part)
    return jnp.concatenate([first, second], axis=axis)


def owner_of(slot, slot_row):
    tiles = jnp.arange(slot_row.shape[0], dtype=jnp.int32)
    return jnp.sum(jnp.where(slot_row == slot, tiles, 0))


def halo_rows(rims, slot_row, my_slot, tz_i, tx_i, n_x):
    column = lax.all_gather(rims, "tz", axis=0, tiled=False)
    received = [None]
    for shift in range(1, n_x):
        dest_tile = tz_i * n_x + (tx_i + shift) % n_x
        dest_slot = lax.dynamic_index_in_dim(slot_row, dest_tile, 0, keepdims=False)
        up_src = owner_of(dest_slot - 1, slot_row)
        down_src = owner_of(dest_slot + 1, slot_row)
        up_part = lax.dynamic_index_in_dim(column, up_src // n_x, 0, keepdims=False)[1]
        down_part = lax.dynamic_index_in_dim(column, down_src // n_x, 0, keepdims=False)[0]
        up_part = jnp.where(up_src % n_x == tx_i, up_part, jnp.zeros_like(up_part))
        down_part = jnp.where(down_src % n_x == tx_i, down_part, jnp.zeros_like(down_part))
        chunk = jnp.stack([up_part, down_part])
        received.append(
            lax.ppermute(chunk, "tx", [(i, (i + shift) % n_x) for i in range(n_x)])
        )
    up_src = owner_of(my_slot - 1, slot_row)
    down_src = owner_of(my_slot + 1, slot_row)
    up_shift = (tx_i - up_src % n_x) % n_x
    down_shift = (tx_i - down_src % n_x) % n_x
    up_own = lax.dynamic_index_in_dim(column, up_src // n_x, 0, keepdims=False)[1]
    down_own = lax.dynamic_index_in_dim(column, down_src // n_x, 0, keepdims=False)[0]
    upper = lax.select_n(up_shift, up_own, *[piece[0] for piece in received[1:]])
    lower = lax.select_n(down_shift, down_own, *[piece[1] for piece in received[1:]])
    return upper, lower


def on_device(
    latent,
    tile_slot,
    tile_count,
    merge_num,
    conv_ema,
    conv_adjusted,
    query_ema,
    query_adjusted,
    kv_ema,
    kv_adjusted,
    out_ema,
    out_adjusted,
    norm_gain,
):
    image_index = lax.axis_index("image")
    tile_index = lax.axis_index("tz") * lax.axis_size("tx") + lax.axis_index("tx")
    slot_row = lax.dynamic_index_in_dim(tile_slot, image_index, 0, keepdims=False)
    live_count = lax.dynamic_index_in_dim(tile_count, image_index, 0, keepdims=False)
    my_slot = lax.dynamic_index_in_dim(slot_row, tile_index, 0, keepdims=False)
    live_flag = (my_slot < live_count).astype(jnp.float32)
    blend_ratio = merge_num[0].astype(jnp.float32) / 16.0

    feats = latent[0]
    tile_rows, chan_shard, tile_cols = feats.shape
    activated = jax.nn.silu(feats.astype(jnp.float32)).astype(jnp.bfloat16)
    rim_rows = jnp.stack([feats[0], feats[-1]])
    n_x = lax.axis_size("tx")
    upper, lower = halo_rows(
        rim_rows, slot_row, my_slot, lax.axis_index("tz"), lax.axis_index("tx"), n_x
    )

    conv_w = image_pair(blend(conv_ema, conv_adjusted, blend_ratio), image_index, 3)
    query_w = image_pair(blend(query_ema, query_adjusted, blend_ratio), image_index, 0)
    kv_w = image_pair(blend(kv_ema, kv_adjusted, blend_ratio), image_index, 0)
    out_w = image_pair(blend(out_ema, out_adjusted, blend_ratio), image_index, 1)
    conv_w = conv_w.reshape(3, 3, -1, conv_w.shape[-1])

    has_upper = my_slot > 0
    has_lower = my_slot + 1 < live_count
    upper = jax.nn.silu(upper.astype(jnp.float32)).astype(jnp.bfloat16)
    lower = jax.nn.silu(lower.astype(jnp.float32)).astype(jnp.bfloat16)
    upper = jnp.where(has_upper, upper, jnp.zeros_like(upper))
    lower = jnp.where(has_lower, lower, jnp.zeros_like(lower))
    block_full = lax.all_gather(activated, "tensor", axis=1, tiled=True)
    conv_inner = convolve(block_full, conv_w, (1, 1))
    halo_full = lax.all_gather(jnp.stack([upper, lower]), "tensor", axis=1, tiled=True)
    up_term = convolve(halo_full[0:1], conv_w[0:1], (0, 0))
    down_term = convolve(halo_full[1:2], conv_w[2:3], (0, 0))
    middle = jnp.zeros((tile_rows - 2,) + up_term.shape[1:], jnp.float32)
    conv_out = conv_inner + jnp.concatenate([up_term, middle, down_term], axis=0)
    section_r = lax.reduce_precision(feats.astype(jnp.float32) + conv_out, exponent_bits=8, mantissa_bits=7)
    section = section_r.astype(jnp.bfloat16)
    section_full = lax.all_gather(section, "tensor", axis=1, tiled=True)
    channels = section_full.shape[1]
    cells = tile_rows * tile_cols
    section_f = section_full.astype(jnp.float32)
    rows_f = jnp.transpose(section_f, (0, 2, 1)).reshape(cells, channels)
    root_mean = jnp.sqrt(jnp.mean(rows_f * rows_f, axis=-1) + 1e-06)
    normed = (rows_f * norm_gain.astype(jnp.float32) / root_mean[:, None]).astype(jnp.bfloat16)
    queries = (jnp.dot(normed, query_w, preferred_element_type=jnp.float32) * HD ** (-0.5)).astype(
        jnp.bfloat16
    )
    att_shard = queries.shape[1]
    head_count = att_shard // HD
    pooled = section_r.reshape(
        tile_rows // POOL, POOL, chan_shard, tile_cols // POOL, POOL
    ).mean(axis=(1, 4))
    tok_count = pooled.shape[0] * pooled.shape[2]
    pooled = jnp.transpose(pooled, (0, 2, 1)).astype(jnp.bfloat16).reshape(tok_count, chan_shard)
    pooled = lax.all_gather(pooled, "tensor", axis=1, tiled=True)
    kv_flat = kv_w.reshape(channels, 2 * att_shard)
    kv_local = jnp.dot(pooled, kv_flat, preferred_element_type=jnp.float32).astype(jnp.bfloat16)
    kv_column = lax.all_gather(kv_local, "tz", axis=0, tiled=False)
    kv_all = lax.all_gather(kv_column, "tx", axis=0, tiled=False)
    n_z = kv_all.shape[1]
    kv_rows = kv_all.reshape(-1, 2 * att_shard)
    key_rows = kv_rows[:, :att_shard]
    key_total = key_rows.shape[0]
    key_tile = (
        jnp.arange(n_x, dtype=jnp.int32)[:, None, None]
        + n_x * jnp.arange(n_z, dtype=jnp.int32)[None, :, None]
        + jnp.zeros((1, 1, tok_count), jnp.int32)
    ).reshape(-1)
    key_live = slot_lookup(key_tile, slot_row) < live_count
    key_livef = key_live.astype(jnp.float32)
    key_heads = key_rows.reshape(key_total, head_count, HD)
    value_heads = kv_rows[:, att_shard:].reshape(key_total, head_count, HD)

    total_list, accum_list = [], []
    for head_index in range(head_count):
        scores = lax.dot_general(
            queries[:, head_index * HD:(head_index + 1) * HD],
            key_heads[:, head_index],
            (((1,), (1,)), ((), ())),
            preferred_element_type=jnp.float32,
        )
        scores = jnp.where(key_live[None, :], scores, -1e30)
        top = jnp.max(scores, axis=1)
        expd = jnp.exp(scores - top[:, None]) * key_livef[None, :]
        total_list.append(jnp.sum(expd, axis=1))
        accum_list.append(
            jnp.dot(
                expd.astype(jnp.bfloat16),
                value_heads[:, head_index],
                preferred_element_type=jnp.float32,
            )
        )
    totals = jnp.stack(total_list, axis=1)
    accum = jnp.stack(accum_list, axis=1)
    attended = (accum / totals[..., None]).astype(jnp.bfloat16).reshape(cells, att_shard)
    attended_stack = lax.all_gather(
        attended.reshape(tile_rows, tile_cols, att_shard), "tensor", axis=0, tiled=False
    )
    projected = jnp.einsum(
        "okj,krwj->row",
        out_w.reshape(chan_shard, -1, att_shard),
        attended_stack,
        preferred_element_type=jnp.float32,
    )
    final = (section_r + projected) * live_flag
    return final.astype(jnp.bfloat16).reshape(1, tile_rows, chan_shard, tile_cols)


def solution(mesh):
    tiles = mesh.shape["tile"]
    inner = 4 if tiles % 4 == 0 else 1
    devices = np.asarray(mesh.devices).reshape(
        (tiles // inner, inner, mesh.shape["image"], mesh.shape["tensor"])
    )
    split = Mesh(devices, ("tz", "tx", "image", "tensor"))
    placed = (
        P("image", TILE_AXES, "tensor", None),
        P(),
        P(),
        P(),
        P(None, None, "tensor", "image", None, None),
        P(None, None, "tensor", "image", None, None),
        P("image", "tensor"),
        P("image", "tensor"),
        P("image", None, "tensor"),
        P("image", None, "tensor"),
        P("tensor", "image"),
        P("tensor", "image"),
        P(),
    )
    return jax.shard_map(
        on_device,
        mesh=split,
        in_specs=placed,
        out_specs=P("image", TILE_AXES, "tensor", None),
        check_vma=False,
    )
```

```python
import numpy as np
import jax
import jax.numpy as jnp
from jax import lax
from jax.sharding import Mesh
from jax.sharding import PartitionSpec as P

HD = 64
POOL = 4
TILE_AXES = ("tz", "tx")


def blend(ema_part, adjusted_part, blend_ratio):
    base = ema_part.astype(jnp.float32)
    return (base + blend_ratio * (adjusted_part.astype(jnp.float32) - base)).astype(jnp.bfloat16)


def convolve(field, kernel, row_padding):
    return lax.conv_general_dilated(
        field[None],
        kernel,
        (1, 1),
        (row_padding, (1, 1)),
        dimension_numbers=("NHCW", "HWOI", "NHCW"),
        preferred_element_type=jnp.float32,
    )[0]


def slot_lookup(tile_ids, slot_row):
    tile_total = slot_row.shape[0]
    matches = tile_ids[:, None] == jnp.arange(tile_total, dtype=jnp.int32)[None, :]
    return jnp.sum(jnp.where(matches, slot_row[None, :], 0), axis=1)


def image_pair(part, image_index, axis):
    other = lax.ppermute(part, "image", [(0, 1), (1, 0)])
    first = jnp.where(image_index == 0, part, other)
    second = jnp.where(image_index == 0, other, part)
    return jnp.concatenate([first, second], axis=axis)


def owner_of(slot, slot_row):
    tiles = jnp.arange(slot_row.shape[0], dtype=jnp.int32)
    return jnp.sum(jnp.where(slot_row == slot, tiles, 0))


def halo_rows(rims, slot_row, my_slot, tz_i, tx_i, n_x):
    column = lax.all_gather(rims, "tz", axis=0, tiled=False)
    received = [None]
    for shift in range(1, n_x):
        dest_tile = tz_i * n_x + (tx_i + shift) % n_x
        dest_slot = lax.dynamic_index_in_dim(slot_row, dest_tile, 0, keepdims=False)
        up_src = owner_of(dest_slot - 1, slot_row)
        down_src = owner_of(dest_slot + 1, slot_row)
        up_part = lax.dynamic_index_in_dim(column, up_src // n_x, 0, keepdims=False)[1]
        down_part = lax.dynamic_index_in_dim(column, down_src // n_x, 0, keepdims=False)[0]
        up_part = jnp.where(up_src % n_x == tx_i, up_part, jnp.zeros_like(up_part))
        down_part = jnp.where(down_src % n_x == tx_i, down_part, jnp.zeros_like(down_part))
        chunk = jnp.stack([up_part, down_part])
        received.append(
            lax.ppermute(chunk, "tx", [(i, (i + shift) % n_x) for i in range(n_x)])
        )
    up_src = owner_of(my_slot - 1, slot_row)
    down_src = owner_of(my_slot + 1, slot_row)
    up_shift = (tx_i - up_src % n_x) % n_x
    down_shift = (tx_i - down_src % n_x) % n_x
    up_own = lax.dynamic_index_in_dim(column, up_src // n_x, 0, keepdims=False)[1]
    down_own = lax.dynamic_index_in_dim(column, down_src // n_x, 0, keepdims=False)[0]
    upper = lax.select_n(up_shift, up_own, *[piece[0] for piece in received[1:]])
    lower = lax.select_n(down_shift, down_own, *[piece[1] for piece in received[1:]])
    return upper, lower


def on_device(
    latent,
    tile_slot,
    tile_count,
    merge_num,
    conv_ema,
    conv_adjusted,
    query_ema,
    query_adjusted,
    kv_ema,
    kv_adjusted,
    out_ema,
    out_adjusted,
    norm_gain,
):
    image_index = lax.axis_index("image")
    tile_index = lax.axis_index("tz") * lax.axis_size("tx") + lax.axis_index("tx")
    slot_row = lax.dynamic_index_in_dim(tile_slot, image_index, 0, keepdims=False)
    live_count = lax.dynamic_index_in_dim(tile_count, image_index, 0, keepdims=False)
    my_slot = lax.dynamic_index_in_dim(slot_row, tile_index, 0, keepdims=False)
    live_flag = (my_slot < live_count).astype(jnp.float32)
    blend_ratio = merge_num[0].astype(jnp.float32) / 16.0

    feats = latent[0]
    tile_rows, chan_shard, tile_cols = feats.shape
    activated = jax.nn.silu(feats.astype(jnp.float32)).astype(jnp.bfloat16)
    rim_rows = jnp.stack([feats[0], feats[-1]])
    n_x = lax.axis_size("tx")
    upper, lower = halo_rows(
        rim_rows, slot_row, my_slot, lax.axis_index("tz"), lax.axis_index("tx"), n_x
    )

    conv_w = image_pair(blend(conv_ema, conv_adjusted, blend_ratio), image_index, 3)
    query_w = image_pair(blend(query_ema, query_adjusted, blend_ratio), image_index, 0)
    kv_w = image_pair(blend(kv_ema, kv_adjusted, blend_ratio), image_index, 0)
    out_w = image_pair(blend(out_ema, out_adjusted, blend_ratio), image_index, 1)
    conv_w = conv_w.reshape(3, 3, -1, conv_w.shape[-1])

    has_upper = my_slot > 0
    has_lower = my_slot + 1 < live_count
    upper = jax.nn.silu(upper.astype(jnp.float32)).astype(jnp.bfloat16)
    lower = jax.nn.silu(lower.astype(jnp.float32)).astype(jnp.bfloat16)
    upper = jnp.where(has_upper, upper, jnp.zeros_like(upper))
    lower = jnp.where(has_lower, lower, jnp.zeros_like(lower))
    block_full = lax.all_gather(activated, "tensor", axis=1, tiled=True)
    conv_inner = convolve(block_full, conv_w, (1, 1))
    halo_stack = lax.all_gather(jnp.stack([upper, lower]), "tensor", axis=0, tiled=False)
    w_halo = conv_w[0::2].reshape(2, 3, chan_shard, halo_stack.shape[0], halo_stack.shape[2])
    taps = jnp.einsum(
        "sbokc,kscw->sbow", w_halo, halo_stack, preferred_element_type=jnp.float32
    )
    edge = jnp.zeros(taps.shape[:1] + taps.shape[2:3] + (1,), jnp.float32)
    halo_terms = (
        jnp.concatenate([edge, taps[:, 0, :, :-1]], axis=-1)
        + taps[:, 1]
        + jnp.concatenate([taps[:, 2, :, 1:], edge], axis=-1)
    )
    up_term, down_term = halo_terms[0:1], halo_terms[1:2]
    middle = jnp.zeros((tile_rows - 2,) + up_term.shape[1:], jnp.float32)
    conv_out = conv_inner + jnp.concatenate([up_term, middle, down_term], axis=0)
    section_r = lax.reduce_precision(feats.astype(jnp.float32) + conv_out, exponent_bits=8, mantissa_bits=7)
    section = section_r.astype(jnp.bfloat16)
    section_full = lax.all_gather(section, "tensor", axis=1, tiled=True)
    channels = section_full.shape[1]
    cells = tile_rows * tile_cols
    section_f = section_full.astype(jnp.float32)
    rows_f = jnp.transpose(section_f, (0, 2, 1)).reshape(cells, channels)
    root_mean = jnp.sqrt(jnp.mean(rows_f * rows_f, axis=-1) + 1e-06)
    normed = (rows_f * norm_gain.astype(jnp.float32) / root_mean[:, None]).astype(jnp.bfloat16)
    queries = (jnp.dot(normed, query_w, preferred_element_type=jnp.float32) * HD ** (-0.5)).astype(
        jnp.bfloat16
    )
    att_shard = queries.shape[1]
    head_count = att_shard // HD
    pooled = section_r.reshape(
        tile_rows // POOL, POOL, chan_shard, tile_cols // POOL, POOL
    ).mean(axis=(1, 4))
    tok_count = pooled.shape[0] * pooled.shape[2]
    pooled = jnp.transpose(pooled, (0, 2, 1)).astype(jnp.bfloat16).reshape(tok_count, chan_shard)
    pooled = lax.all_gather(pooled, "tensor", axis=1, tiled=True)
    kv_flat = kv_w.reshape(channels, 2 * att_shard)
    kv_local = jnp.dot(pooled, kv_flat, preferred_element_type=jnp.float32).astype(jnp.bfloat16)
    kv_column = lax.all_gather(kv_local, "tz", axis=0, tiled=False)
    kv_all = lax.all_gather(kv_column, "tx", axis=0, tiled=False)
    n_z = kv_all.shape[1]
    kv_rows = kv_all.reshape(-1, 2 * att_shard)
    key_rows = kv_rows[:, :att_shard]
    key_total = key_rows.shape[0]
    key_tile = (
        jnp.arange(n_x, dtype=jnp.int32)[:, None, None]
        + n_x * jnp.arange(n_z, dtype=jnp.int32)[None, :, None]
        + jnp.zeros((1, 1, tok_count), jnp.int32)
    ).reshape(-1)
    key_live = slot_lookup(key_tile, slot_row) < live_count
    key_livef = key_live.astype(jnp.float32)
    key_heads = key_rows.reshape(key_total, head_count, HD)
    value_heads = kv_rows[:, att_shard:].reshape(key_total, head_count, HD)

    total_list, accum_list = [], []
    for head_index in range(head_count):
        scores = lax.dot_general(
            queries[:, head_index * HD:(head_index + 1) * HD],
            key_heads[:, head_index],
            (((1,), (1,)), ((), ())),
            preferred_element_type=jnp.float32,
        )
        scores = jnp.where(key_live[None, :], scores, -1e30)
        top = jnp.max(scores, axis=1)
        expd = jnp.exp(scores - top[:, None]) * key_livef[None, :]
        total_list.append(jnp.sum(expd, axis=1))
        accum_list.append(
            jnp.dot(
                expd.astype(jnp.bfloat16),
                value_heads[:, head_index],
                preferred_element_type=jnp.float32,
            )
        )
    totals = jnp.stack(total_list, axis=1)
    accum = jnp.stack(accum_list, axis=1)
    attended = (accum / totals[..., None]).astype(jnp.bfloat16).reshape(cells, att_shard)
    attended_full = lax.all_gather(attended, "tensor", axis=1, tiled=True)
    projected = lax.dot_general(
        out_w, attended_full, (((1,), (1,)), ((), ())), preferred_element_type=jnp.float32
    )
    projected = jnp.transpose(projected.reshape(chan_shard, tile_rows, tile_cols), (1, 0, 2))
    final = (section_r + projected) * live_flag
    return final.astype(jnp.bfloat16).reshape(1, tile_rows, chan_shard, tile_cols)


def solution(mesh):
    tiles = mesh.shape["tile"]
    inner = 4 if tiles % 4 == 0 else 1
    devices = np.asarray(mesh.devices).reshape(
        (tiles // inner, inner, mesh.shape["image"], mesh.shape["tensor"])
    )
    split = Mesh(devices, ("tz", "tx", "image", "tensor"))
    placed = (
        P("image", TILE_AXES, "tensor", None),
        P(),
        P(),
        P(),
        P(None, None, "tensor", "image", None, None),
        P(None, None, "tensor", "image", None, None),
        P("image", "tensor"),
        P("image", "tensor"),
        P("image", None, "tensor"),
        P("image", None, "tensor"),
        P("tensor", "image"),
        P("tensor", "image"),
        P(),
    )
    return jax.shard_map(
        on_device,
        mesh=split,
        in_specs=placed,
        out_specs=P("image", TILE_AXES, "tensor", None),
        check_vma=False,
    )
```

```python
import numpy as np
import jax
import jax.numpy as jnp
from jax import lax
from jax.sharding import Mesh
from jax.sharding import PartitionSpec as P

HD = 64
POOL = 4
TILE_AXES = ("tz", "tx")


def blend(ema_part, adjusted_part, blend_ratio):
    base = ema_part.astype(jnp.float32)
    return (base + blend_ratio * (adjusted_part.astype(jnp.float32) - base)).astype(jnp.bfloat16)


def convolve(field, kernel, row_padding):
    return lax.conv_general_dilated(
        field[None],
        kernel,
        (1, 1),
        (row_padding, (1, 1)),
        dimension_numbers=("NHCW", "HWOI", "NHCW"),
        preferred_element_type=jnp.float32,
    )[0]


def slot_lookup(tile_ids, slot_row):
    tile_total = slot_row.shape[0]
    matches = tile_ids[:, None] == jnp.arange(tile_total, dtype=jnp.int32)[None, :]
    return jnp.sum(jnp.where(matches, slot_row[None, :], 0), axis=1)


def image_pair(part, image_index, axis):
    other = lax.ppermute(part, "image", [(0, 1), (1, 0)])
    first = jnp.where(image_index == 0, part, other)
    second = jnp.where(image_index == 0, other, part)
    return jnp.concatenate([first, second], axis=axis)


def owner_of(slot, slot_row):
    tiles = jnp.arange(slot_row.shape[0], dtype=jnp.int32)
    return jnp.sum(jnp.where(slot_row == slot, tiles, 0))


def halo_rows(rims, slot_row, my_slot, tz_i, tx_i, n_x):
    column = lax.all_gather(rims, "tz", axis=0, tiled=False)
    received = [None]
    for shift in range(1, n_x):
        dest_tile = tz_i * n_x + (tx_i + shift) % n_x
        dest_slot = lax.dynamic_index_in_dim(slot_row, dest_tile, 0, keepdims=False)
        up_src = owner_of(dest_slot - 1, slot_row)
        down_src = owner_of(dest_slot + 1, slot_row)
        up_part = lax.dynamic_index_in_dim(column, up_src // n_x, 0, keepdims=False)[1]
        down_part = lax.dynamic_index_in_dim(column, down_src // n_x, 0, keepdims=False)[0]
        up_part = jnp.where(up_src % n_x == tx_i, up_part, jnp.zeros_like(up_part))
        down_part = jnp.where(down_src % n_x == tx_i, down_part, jnp.zeros_like(down_part))
        chunk = jnp.stack([up_part, down_part])
        received.append(
            lax.ppermute(chunk, "tx", [(i, (i + shift) % n_x) for i in range(n_x)])
        )
    up_src = owner_of(my_slot - 1, slot_row)
    down_src = owner_of(my_slot + 1, slot_row)
    up_shift = (tx_i - up_src % n_x) % n_x
    down_shift = (tx_i - down_src % n_x) % n_x
    up_own = lax.dynamic_index_in_dim(column, up_src // n_x, 0, keepdims=False)[1]
    down_own = lax.dynamic_index_in_dim(column, down_src // n_x, 0, keepdims=False)[0]
    upper = lax.select_n(up_shift, up_own, *[piece[0] for piece in received[1:]])
    lower = lax.select_n(down_shift, down_own, *[piece[1] for piece in received[1:]])
    return upper, lower


def on_device(
    latent,
    tile_slot,
    tile_count,
    merge_num,
    conv_ema,
    conv_adjusted,
    query_ema,
    query_adjusted,
    kv_ema,
    kv_adjusted,
    out_ema,
    out_adjusted,
    norm_gain,
):
    image_index = lax.axis_index("image")
    tile_index = lax.axis_index("tz") * lax.axis_size("tx") + lax.axis_index("tx")
    slot_row = lax.dynamic_index_in_dim(tile_slot, image_index, 0, keepdims=False)
    live_count = lax.dynamic_index_in_dim(tile_count, image_index, 0, keepdims=False)
    my_slot = lax.dynamic_index_in_dim(slot_row, tile_index, 0, keepdims=False)
    live_flag = (my_slot < live_count).astype(jnp.float32)
    blend_ratio = merge_num[0].astype(jnp.float32) / 16.0

    feats = latent[0]
    tile_rows, chan_shard, tile_cols = feats.shape
    activated = jax.nn.silu(feats.astype(jnp.float32)).astype(jnp.bfloat16)
    rim_rows = jnp.stack([feats[0], feats[-1]])
    n_x = lax.axis_size("tx")
    upper, lower = halo_rows(
        rim_rows, slot_row, my_slot, lax.axis_index("tz"), lax.axis_index("tx"), n_x
    )

    conv_w = image_pair(blend(conv_ema, conv_adjusted, blend_ratio), image_index, 3)
    query_w = image_pair(blend(query_ema, query_adjusted, blend_ratio), image_index, 0)
    kv_w = image_pair(blend(kv_ema, kv_adjusted, blend_ratio), image_index, 0)
    out_w = image_pair(blend(out_ema, out_adjusted, blend_ratio), image_index, 1)
    conv_w = conv_w.reshape(3, 3, -1, conv_w.shape[-1])

    has_upper = my_slot > 0
    has_lower = my_slot + 1 < live_count
    upper = jax.nn.silu(upper.astype(jnp.float32)).astype(jnp.bfloat16)
    lower = jax.nn.silu(lower.astype(jnp.float32)).astype(jnp.bfloat16)
    upper = jnp.where(has_upper, upper, jnp.zeros_like(upper))
    lower = jnp.where(has_lower, lower, jnp.zeros_like(lower))
    block_full = lax.all_gather(activated, "tensor", axis=1, tiled=True)
    conv_inner = convolve(block_full, conv_w, (1, 1))
    halo_full = lax.all_gather(jnp.stack([upper, lower]), "tensor", axis=1, tiled=True)
    up_term = convolve(halo_full[0:1], conv_w[0:1], (0, 0))
    down_term = convolve(halo_full[1:2], conv_w[2:3], (0, 0))
    middle = jnp.zeros((tile_rows - 2,) + up_term.shape[1:], jnp.float32)
    conv_out = conv_inner + jnp.concatenate([up_term, middle, down_term], axis=0)
    section_r = lax.reduce_precision(feats.astype(jnp.float32) + conv_out, exponent_bits=8, mantissa_bits=7)
    section = section_r.astype(jnp.bfloat16)
    section_full = lax.all_gather(section, "tensor", axis=1, tiled=True)
    channels = section_full.shape[1]
    cells = tile_rows * tile_cols
    section_f = section_full.astype(jnp.float32)
    rows_f = jnp.transpose(section_f, (0, 2, 1)).reshape(cells, channels)
    root_mean = jnp.sqrt(jnp.mean(rows_f * rows_f, axis=-1) + 1e-06)
    normed = (rows_f * norm_gain.astype(jnp.float32) / root_mean[:, None]).astype(jnp.bfloat16)
    queries = (jnp.dot(normed, query_w, preferred_element_type=jnp.float32) * HD ** (-0.5)).astype(
        jnp.bfloat16
    )
    att_shard = queries.shape[1]
    head_count = att_shard // HD
    pooled = section_r.reshape(
        tile_rows // POOL, POOL, chan_shard, tile_cols // POOL, POOL
    ).mean(axis=(1, 4))
    tok_count = pooled.shape[0] * pooled.shape[2]
    pooled = jnp.transpose(pooled, (0, 2, 1)).astype(jnp.bfloat16).reshape(tok_count, chan_shard)
    pooled = lax.all_gather(pooled, "tensor", axis=0, tiled=False)
    kv_flat = kv_w.reshape(channels, 2 * att_shard)
    kv_local = jnp.einsum(
        "ktc,kcj->tj",
        pooled,
        kv_flat.reshape(pooled.shape[0], chan_shard, -1),
        preferred_element_type=jnp.float32,
    ).astype(jnp.bfloat16)
    kv_column = lax.all_gather(kv_local, "tz", axis=0, tiled=False)
    kv_all = lax.all_gather(kv_column, "tx", axis=0, tiled=False)
    n_z = kv_all.shape[1]
    kv_rows = kv_all.reshape(-1, 2 * att_shard)
    key_rows = kv_rows[:, :att_shard]
    key_total = key_rows.shape[0]
    key_tile = (
        jnp.arange(n_x, dtype=jnp.int32)[:, None, None]
        + n_x * jnp.arange(n_z, dtype=jnp.int32)[None, :, None]
        + jnp.zeros((1, 1, tok_count), jnp.int32)
    ).reshape(-1)
    key_live = slot_lookup(key_tile, slot_row) < live_count
    key_livef = key_live.astype(jnp.float32)
    key_heads = key_rows.reshape(key_total, head_count, HD)
    value_heads = kv_rows[:, att_shard:].reshape(key_total, head_count, HD)

    total_list, accum_list = [], []
    for head_index in range(head_count):
        scores = lax.dot_general(
            queries[:, head_index * HD:(head_index + 1) * HD],
            key_heads[:, head_index],
            (((1,), (1,)), ((), ())),
            preferred_element_type=jnp.float32,
        )
        scores = jnp.where(key_live[None, :], scores, -1e30)
        top = jnp.max(scores, axis=1)
        expd = jnp.exp(scores - top[:, None]) * key_livef[None, :]
        total_list.append(jnp.sum(expd, axis=1))
        accum_list.append(
            jnp.dot(
                expd.astype(jnp.bfloat16),
                value_heads[:, head_index],
                preferred_element_type=jnp.float32,
            )
        )
    totals = jnp.stack(total_list, axis=1)
    accum = jnp.stack(accum_list, axis=1)
    attended = (accum / totals[..., None]).astype(jnp.bfloat16).reshape(cells, att_shard)
    attended_full = lax.all_gather(attended, "tensor", axis=1, tiled=True)
    projected = lax.dot_general(
        out_w, attended_full, (((1,), (1,)), ((), ())), preferred_element_type=jnp.float32
    )
    projected = jnp.transpose(projected.reshape(chan_shard, tile_rows, tile_cols), (1, 0, 2))
    final = (section_r + projected) * live_flag
    return final.astype(jnp.bfloat16).reshape(1, tile_rows, chan_shard, tile_cols)


def solution(mesh):
    tiles = mesh.shape["tile"]
    inner = 4 if tiles % 4 == 0 else 1
    devices = np.asarray(mesh.devices).reshape(
        (tiles // inner, inner, mesh.shape["image"], mesh.shape["tensor"])
    )
    split = Mesh(devices, ("tz", "tx", "image", "tensor"))
    placed = (
        P("image", TILE_AXES, "tensor", None),
        P(),
        P(),
        P(),
        P(None, None, "tensor", "image", None, None),
        P(None, None, "tensor", "image", None, None),
        P("image", "tensor"),
        P("image", "tensor"),
        P("image", None, "tensor"),
        P("image", None, "tensor"),
        P("tensor", "image"),
        P("tensor", "image"),
        P(),
    )
    return jax.shard_map(
        on_device,
        mesh=split,
        in_specs=placed,
        out_specs=P("image", TILE_AXES, "tensor", None),
        check_vma=False,
    )
```
